128 devices in a mesh: ctx: 8 (over z, x_hi), head: 16 (over x_lo, y, core).
Axes of the slice: x: 4 (x_hi: 2, x_lo: 2; x = x_hi * 2 + x_lo), y: 4, z: 4, core: 2. Of those that a mesh axis runs over, the one named last changes fastest.
Arguments:
- queries: bfloat16 [32768, 4096], P(('ctx', 'head')), may hold values from -8 to 8
- keys: bfloat16 [32768, 2048], P(('ctx', 'head')), may hold values from -8 to 8
- values: bfloat16 [32768, 2048], P(('ctx', 'head')), may hold values from -18 to 18
- grad_out: bfloat16 [32768, 4096], P(('ctx', 'head')), may hold values from -18 to 18
Outputs:
- attended: bfloat16 [32768, 4096], P(('ctx', 'head'))
- grad_queries: bfloat16 [32768, 4096], P(('ctx', 'head'))
- grad_keys: bfloat16 [32768, 2048], P(('ctx', 'head'))
- grad_values: bfloat16 [32768, 2048], P(('ctx', 'head'))
The draws below stay inside these ranges and needn't reach their ends.
All inputs are finite; a program needn't handle non-finite values.
Results may differ from the reference program's by a relative error of at most 0.02.
Values may be sent and summed in bfloat16 or wider, within the bound.
No kernel may reach another device: no remote copies, remote signals or barrier semaphores. Data moves between devices by JAX's collectives and lax.ppermute only.
A program may use at most 256 MiB of HBM per device.

```python
import jax
import jax.numpy as jnp
from jax import lax

HD = 128
QH = 32
KVH = 16
WIN = 1024
QPRE = 168
BLK = 256
SEQ = 32768


def draw_queries(key, part):
    base_rows = jnp.clip(2.0 * jax.random.normal(jax.random.fold_in(key, 3), (SEQ, QH, HD), jnp.float32), -8.0, 8.0)
    return base_rows.reshape(SEQ, QH * HD).astype(jnp.bfloat16)


def draw_keys(key, part):
    base_rows = jnp.clip(jax.random.normal(jax.random.fold_in(key, 4), (SEQ, KVH, HD), jnp.float32), -6.0, 6.0)
    return base_rows.reshape(SEQ, KVH * HD).astype(jnp.bfloat16)


def block_scale(rng, shape, pieces, smallest, high):
    loudness = 1.0
    for dim, parts in pieces:
        heights = jax.random.uniform(jax.random.fold_in(jax.random.fold_in(rng, 6), dim), (parts,), jnp.float32, smallest / len(pieces), high / len(pieces))
        loudness = loudness * jnp.repeat(jnp.exp(heights), shape[dim] // parts).reshape((-1,) + (1,) * (len(shape) - 1 - dim))
    return loudness


def normal_values(rng, extent, scale, bound, cuts=(), kind=jnp.bfloat16):
    values = scale * jax.random.normal(rng, extent, jnp.float32)
    if cuts:
        values = values * block_scale(rng, extent, cuts, -0.22, 0.18)
    return jnp.clip(values, -bound, bound).astype(kind)


def setup_inputs(seed: int = 0) -> dict:
    key_list = jax.random.split(jax.random.key(seed), 5)
    queries = draw_queries(jax.random.fold_in(key_list[4], 71), 0)
    keys = draw_keys(jax.random.fold_in(key_list[4], 71), 0)
    values = normal_values(key_list[2], (SEQ, KVH * HD), 3.0, 18.0, ((0, 128),))
    grad_out = normal_values(key_list[3], (SEQ, QH * HD), 3.0, 18.0, ((0, 128),))
    return {"queries": queries, "keys": keys, "values": values, "grad_out": grad_out}


def arrange(block, shared_heads, group_size):
    rows = block.shape[0]
    width = block.shape[2]
    stacked = block.reshape(rows, shared_heads, group_size, width)
    return jnp.transpose(stacked, (1, 2, 0, 3)).reshape(shared_heads, group_size * rows, width)


def restore(stack, rows, group_size):
    shared_heads = stack.shape[0]
    width = stack.shape[2]
    split = stack.reshape(shared_heads, group_size, rows, width)
    return jnp.transpose(split, (2, 0, 1, 3)).reshape(rows, shared_heads * group_size, width)


def attend(queries, keys_ext, values_ext, grads, first_query):
    query_count = queries.shape[0]
    query_heads = queries.shape[1]
    shared_heads = keys_ext.shape[1]
    head_width = queries.shape[2]
    group_size = query_heads // shared_heads
    block_rows = min(BLK, query_count)
    key_span = WIN + block_rows
    block_total = query_count // block_rows
    scale = QPRE ** -0.5

    def block_step(totals, block):
        key_total, value_total = totals
        first_row = block * block_rows
        query_block = lax.dynamic_slice_in_dim(queries, first_row, block_rows, 0)
        grad_block = lax.dynamic_slice_in_dim(grads, first_row, block_rows, 0)
        key_block = lax.dynamic_slice_in_dim(keys_ext, first_row, key_span, 0)
        value_block = lax.dynamic_slice_in_dim(values_ext, first_row, key_span, 0)
        query_pos = first_query + first_row + jnp.arange(block_rows, dtype=jnp.int32)
        key_pos = first_query - WIN + first_row + jnp.arange(key_span, dtype=jnp.int32)
        distance = query_pos[:, None] - key_pos[None, :]
        allowed = (distance >= 0) & (distance < WIN) & (key_pos[None, :] >= 0)
        allowed = jnp.tile(allowed, (group_size, 1))
        query_stack = arrange(query_block, shared_heads, group_size).astype(jnp.float32)
        grad_stack = arrange(grad_block, shared_heads, group_size).astype(jnp.float32)
        key_stack = jnp.transpose(key_block, (1, 0, 2)).astype(jnp.float32)
        value_stack = jnp.transpose(value_block, (1, 0, 2)).astype(jnp.float32)
        scores = jnp.einsum("hqd,hkd->hqk", query_stack, key_stack) * scale
        scores = jnp.where(allowed[None], scores, -jnp.inf)
        largest = jnp.max(scores, axis=-1, keepdims=True)
        unnormed = jnp.exp(scores - largest)
        probs = unnormed / jnp.sum(unnormed, axis=-1, keepdims=True)
        probs_low = probs.astype(jnp.bfloat16)
        output_stack = jnp.einsum("hqk,hkd->hqd", probs_low.astype(jnp.float32), value_stack).astype(jnp.bfloat16)
        grad_probs = jnp.einsum("hqd,hkd->hqk", grad_stack, value_stack)
        inner = jnp.sum(grad_stack * output_stack.astype(jnp.float32), axis=-1, keepdims=True)
        grad_scores = (probs * (grad_probs - inner) * scale).astype(jnp.bfloat16)
        grad_query = jnp.einsum("hqk,hkd->hqd", grad_scores.astype(jnp.float32), key_stack).astype(jnp.bfloat16)
        grad_key = jnp.einsum("hqk,hqd->khd", grad_scores.astype(jnp.float32), query_stack)
        grad_value = jnp.einsum("hqk,hqd->khd", probs_low.astype(jnp.float32), grad_stack)
        key_old = lax.dynamic_slice_in_dim(key_total, first_row, key_span, 0)
        value_old = lax.dynamic_slice_in_dim(value_total, first_row, key_span, 0)
        key_total = lax.dynamic_update_slice_in_dim(key_total, key_old + grad_key, first_row, 0)
        value_total = lax.dynamic_update_slice_in_dim(value_total, value_old + grad_value, first_row, 0)
        return (key_total, value_total), (restore(output_stack, block_rows, group_size), restore(grad_query, block_rows, group_size))

    zeros_ext = jnp.zeros((WIN + query_count, shared_heads, head_width), jnp.float32)
    (key_total, value_total), (outputs, grad_queries) = lax.scan(block_step, (zeros_ext, zeros_ext), jnp.arange(block_total, dtype=jnp.int32))
    attended = outputs.reshape(query_count, query_heads, head_width)
    grad_queries = grad_queries.reshape(query_count, query_heads, head_width)
    return attended, grad_queries, key_total, value_total


def reference(queries, keys, values, grad_out):
    query_rows = queries.reshape(SEQ, QH, HD)
    key_rows = keys.reshape(SEQ, KVH, HD)
    value_rows = values.reshape(SEQ, KVH, HD)
    grad_rows = grad_out.reshape(SEQ, QH, HD)
    padding = jnp.zeros((WIN, KVH, HD), keys.dtype)
    keys_ext = jnp.concatenate([padding, key_rows], axis=0)
    values_ext = jnp.concatenate([padding, value_rows], axis=0)
    attended, grad_queries, key_total, value_total = attend(query_rows, keys_ext, values_ext, grad_rows, 0)
    grad_keys = key_total[WIN:].astype(jnp.bfloat16)
    grad_values = value_total[WIN:].astype(jnp.bfloat16)
    return (attended.reshape(SEQ, QH * HD), grad_queries.reshape(SEQ, QH * HD), grad_keys.reshape(SEQ, KVH * HD), grad_values.reshape(SEQ, KVH * HD))
```

```python
import functools

import jax
import jax.numpy as jnp
from jax import lax
from jax.experimental import pallas as pl
from jax.experimental.pallas import tpu as pltpu
from jax.sharding import PartitionSpec as P

HD = 128
QH = 32
KVH = 16
WIN = 1024
QPRE = 168
BLK = 256


def shifted(block, axis, distance):
    devices = range(lax.axis_size(axis))
    route = [(i - distance, i) for i in devices if i - distance in devices]
    return lax.ppermute(block, axis, route)


def attend_kernel(first_ref, q_ref, g_ref, k_ref, v_ref, o_ref, dq_ref, dk_ref, dv_ref):
    block = pl.program_id(0)
    rows = q_ref.shape[0]
    group = q_ref.shape[1] // HD
    span = WIN + rows
    scale = QPRE ** (-0.5)

    @pl.when(block == 0)
    def _():
        dk_ref[...] = jnp.zeros_like(dk_ref)
        dv_ref[...] = jnp.zeros_like(dv_ref)

    start = pl.multiple_of(block * rows, rows)
    k_win = k_ref[pl.ds(start, span), :]
    v_win = v_ref[pl.ds(start, span), :]
    row_id = lax.broadcasted_iota(jnp.int32, (rows, span), 0)
    col_id = lax.broadcasted_iota(jnp.int32, (rows, span), 1)
    distance = row_id + WIN - col_id
    key_pos = first_ref[0] - WIN + start + col_id
    allowed = (distance >= 0) & (distance < WIN) & (key_pos >= 0)
    dk_acc = jnp.zeros((span, HD), jnp.float32)
    dv_acc = jnp.zeros((span, HD), jnp.float32)
    nt = (((1,), (1,)), ((), ()))
    tn = (((0,), (0,)), ((), ()))
    for h in range(group):
        q = q_ref[:, h * HD:(h + 1) * HD]
        g = g_ref[:, h * HD:(h + 1) * HD]
        scores = lax.dot_general(q, k_win, nt, preferred_element_type=jnp.float32) * scale
        scores = jnp.where(allowed, scores, -jnp.inf)
        largest = jnp.max(scores, axis=-1, keepdims=True)
        unnormed = jnp.exp(scores - largest)
        probs = unnormed / jnp.sum(unnormed, axis=-1, keepdims=True)
        probs_low = probs.astype(jnp.bfloat16)
        out = jnp.dot(probs_low, v_win, preferred_element_type=jnp.float32).astype(jnp.bfloat16)
        o_ref[:, h * HD:(h + 1) * HD] = out
        grad_probs = lax.dot_general(g, v_win, nt, preferred_element_type=jnp.float32)
        inner = jnp.sum(g.astype(jnp.float32) * out.astype(jnp.float32), axis=-1, keepdims=True)
        grad_scores = (probs * (grad_probs - inner) * scale).astype(jnp.bfloat16)
        dq_ref[:, h * HD:(h + 1) * HD] = jnp.dot(
            grad_scores, k_win, preferred_element_type=jnp.float32
        ).astype(jnp.bfloat16)
        dk_acc = dk_acc + lax.dot_general(grad_scores, q, tn, preferred_element_type=jnp.float32)
        dv_acc = dv_acc + lax.dot_general(probs_low, g, tn, preferred_element_type=jnp.float32)
    dk_ref[pl.ds(start, span), :] += dk_acc
    dv_ref[pl.ds(start, span), :] += dv_acc


def attend(queries, keys_ext, values_ext, grads, first_query):
    query_count, width = queries.shape
    ext_rows = keys_ext.shape[0]
    rows = BLK
    block_total = query_count // rows
    first = jnp.reshape(first_query, (1,)).astype(jnp.int32)
    grid_spec = pltpu.PrefetchScalarGridSpec(
        num_scalar_prefetch=1,
        grid=(block_total,),
        in_specs=[
            pl.BlockSpec((rows, width), lambda b, f: (b, 0)),
            pl.BlockSpec((rows, width), lambda b, f: (b, 0)),
            pl.BlockSpec((ext_rows, HD), lambda b, f: (0, 0)),
            pl.BlockSpec((ext_rows, HD), lambda b, f: (0, 0)),
        ],
        out_specs=[
            pl.BlockSpec((rows, width), lambda b, f: (b, 0)),
            pl.BlockSpec((rows, width), lambda b, f: (b, 0)),
            pl.BlockSpec((ext_rows, HD), lambda b, f: (0, 0)),
            pl.BlockSpec((ext_rows, HD), lambda b, f: (0, 0)),
        ],
    )
    return pl.pallas_call(
        attend_kernel,
        grid_spec=grid_spec,
        out_shape=[
            jax.ShapeDtypeStruct((query_count, width), jnp.bfloat16),
            jax.ShapeDtypeStruct((query_count, width), jnp.bfloat16),
            jax.ShapeDtypeStruct((ext_rows, HD), jnp.float32),
            jax.ShapeDtypeStruct((ext_rows, HD), jnp.float32),
        ],
        compiler_params=pltpu.CompilerParams(
            dimension_semantics=("arbitrary",), vmem_limit_bytes=56 * 1024 * 1024
        ),
    )(first, queries, grads, keys_ext, values_ext)


def body(queries, keys, values, grad_out):
    token_count = queries.shape[0]
    query_rows = queries.reshape(token_count, QH, HD)
    key_rows = keys.reshape(token_count, KVH, HD)
    value_rows = values.reshape(token_count, KVH, HD)
    grad_rows = grad_out.reshape(token_count, QH, HD)
    group_queries, group_keys, group_values, group_grads = (
        lax.all_to_all(query_rows, "head", split_axis=1, concat_axis=0, tiled=True),
        lax.all_to_all(key_rows, "head", split_axis=1, concat_axis=0, tiled=True),
        lax.all_to_all(value_rows, "head", split_axis=1, concat_axis=0, tiled=True),
        lax.all_to_all(grad_rows, "head", split_axis=1, concat_axis=0, tiled=True),
    )
    group_rows = group_queries.shape[0]
    query_heads = group_queries.shape[1]
    first_query = lax.axis_index("ctx") * group_rows
    group_keys = group_keys.reshape(group_rows, HD)
    group_values = group_values.reshape(group_rows, HD)
    key_tail, value_tail = shifted(
        (group_keys[group_rows - WIN :], group_values[group_rows - WIN :]), "ctx", 1
    )
    keys_ext = jnp.concatenate([key_tail, group_keys], axis=0)
    values_ext = jnp.concatenate([value_tail, group_values], axis=0)
    attended_group, grad_query_group, key_total, value_total = attend(
        group_queries.reshape(group_rows, query_heads * HD),
        keys_ext,
        values_ext,
        group_grads.reshape(group_rows, query_heads * HD),
        first_query,
    )
    key_back, value_back = (
        shifted(key_total[:WIN].astype(jnp.bfloat16), "ctx", -1).astype(jnp.float32),
        shifted(value_total[:WIN].astype(jnp.bfloat16), "ctx", -1).astype(jnp.float32),
    )
    key_grad = jnp.concatenate(
        [key_total[WIN:group_rows], key_total[group_rows:] + key_back], axis=0
    ).astype(jnp.bfloat16)
    value_grad = jnp.concatenate(
        [value_total[WIN:group_rows], value_total[group_rows:] + value_back], axis=0
    ).astype(jnp.bfloat16)
    attended_group = attended_group.reshape(group_rows, query_heads, HD)
    grad_query_group = grad_query_group.reshape(group_rows, query_heads, HD)
    key_grad = key_grad.reshape(group_rows, 1, HD)
    value_grad = value_grad.reshape(group_rows, 1, HD)
    attended, grad_queries, key_out, value_out = (
        lax.all_to_all(attended_group, "head", split_axis=0, concat_axis=1, tiled=True),
        lax.all_to_all(grad_query_group, "head", split_axis=0, concat_axis=1, tiled=True),
        lax.all_to_all(key_grad, "head", split_axis=0, concat_axis=1, tiled=True),
        lax.all_to_all(value_grad, "head", split_axis=0, concat_axis=1, tiled=True),
    )
    return (
        attended.reshape(token_count, QH * HD),
        grad_queries.reshape(token_count, QH * HD),
        key_out.reshape(token_count, KVH * HD),
        value_out.reshape(token_count, KVH * HD),
    )


def solution(mesh):
    placed = (
        P(("ctx", "head"), None),
        P(("ctx", "head"), None),
        P(("ctx", "head"), None),
        P(("ctx", "head"), None),
    )
    return jax.shard_map(
        body,
        mesh=mesh,
        in_specs=placed,
        out_specs=(
            P(("ctx", "head"), None),
            P(("ctx", "head"), None),
            P(("ctx", "head"), None),
            P(("ctx", "head"), None),
        ),
        check_vma=False,
    )
```

```python
import functools

import jax
import jax.numpy as jnp
from jax import lax
from jax.experimental import pallas as pl
from jax.experimental.pallas import tpu as pltpu
from jax.sharding import PartitionSpec as P

HD = 128
QH = 32
KVH = 16
WIN = 1024
QPRE = 168
BLK = 256


def shifted(block, axis, distance):
    devices = range(lax.axis_size(axis))
    route = [(i - distance, i) for i in devices if i - distance in devices]
    return lax.ppermute(block, axis, route)


def attend_kernel(first_ref, q_ref, g_ref, k_ref, v_ref, *rest):
    if len(rest) == 5:
        dk_in_ref, dv_in_ref, od_ref, dk_ref, dv_ref = rest
    else:
        dk_in_ref = dv_in_ref = None
        od_ref, dk_ref, dv_ref = rest
    block = pl.program_id(0)
    rows = q_ref.shape[0]
    span = WIN + rows
    scale = QPRE ** (-0.5)

    @pl.when(block == 0)
    def _():
        if dk_in_ref is None:
            dk_ref[...] = jnp.zeros_like(dk_ref)
            dv_ref[...] = jnp.zeros_like(dv_ref)
        else:
            dk_ref[...] = dk_in_ref[...]
            dv_ref[...] = dv_in_ref[...]

    start = pl.multiple_of(block * rows, rows)
    k_win = k_ref[pl.ds(start, span), :]
    v_win = v_ref[pl.ds(start, span), :]
    row_id = lax.broadcasted_iota(jnp.int32, (rows, span), 0)
    col_id = lax.broadcasted_iota(jnp.int32, (rows, span), 1)
    distance = row_id + WIN - col_id
    key_pos = first_ref[0] - WIN + start + col_id
    allowed = (distance >= 0) & (distance < WIN) & (key_pos >= 0)
    nt = (((1,), (1,)), ((), ()))
    tn = (((0,), (0,)), ((), ()))
    q = q_ref[...]
    g = g_ref[...]
    scores = lax.dot_general(q, k_win, nt, preferred_element_type=jnp.float32) * scale
    scores = jnp.where(allowed, scores, -jnp.inf)
    largest = jnp.max(scores, axis=-1, keepdims=True)
    unnormed = jnp.exp(scores - largest)
    probs = unnormed / jnp.sum(unnormed, axis=-1, keepdims=True)
    probs_low = probs.astype(jnp.bfloat16)
    out = jnp.dot(probs_low, v_win, preferred_element_type=jnp.float32).astype(jnp.bfloat16)
    od_ref[:, :HD] = out
    grad_probs = lax.dot_general(g, v_win, nt, preferred_element_type=jnp.float32)
    inner = jnp.sum(g.astype(jnp.float32) * out.astype(jnp.float32), axis=-1, keepdims=True)
    grad_scores = (probs * (grad_probs - inner) * scale).astype(jnp.bfloat16)
    od_ref[:, HD:] = jnp.dot(grad_scores, k_win, preferred_element_type=jnp.float32).astype(
        jnp.bfloat16
    )
    dk_ref[pl.ds(start, span), :] += lax.dot_general(
        grad_scores, q, tn, preferred_element_type=jnp.float32
    )
    dv_ref[pl.ds(start, span), :] += lax.dot_general(
        probs_low, g, tn, preferred_element_type=jnp.float32
    )


def attend(source, q_col, g_col, keys_ext, values_ext, first_query, key_acc=None, value_acc=None):
    query_count = source.shape[0]
    ext_rows = keys_ext.shape[0]
    rows = BLK
    block_total = query_count // rows
    first = jnp.reshape(first_query, (1,)).astype(jnp.int32)
    whole = pl.BlockSpec((ext_rows, HD), lambda b, f: (0, 0))
    in_specs = [
        pl.BlockSpec((rows, HD), lambda b, f: (b, q_col)),
        pl.BlockSpec((rows, HD), lambda b, f: (b, g_col)),
        whole,
        whole,
    ]
    operands = [first, source, source, keys_ext, values_ext]
    aliases = {}
    if key_acc is not None:
        in_specs += [whole, whole]
        operands += [key_acc, value_acc]
        aliases = {5: 1, 6: 2}
    grid_spec = pltpu.PrefetchScalarGridSpec(
        num_scalar_prefetch=1,
        grid=(block_total,),
        in_specs=in_specs,
        out_specs=[pl.BlockSpec((rows, 2 * HD), lambda b, f: (b, 0)), whole, whole],
    )
    return pl.pallas_call(
        attend_kernel,
        grid_spec=grid_spec,
        out_shape=[
            jax.ShapeDtypeStruct((query_count, 2 * HD), jnp.bfloat16),
            jax.ShapeDtypeStruct((ext_rows, HD), jnp.float32),
            jax.ShapeDtypeStruct((ext_rows, HD), jnp.float32),
        ],
        input_output_aliases=aliases,
        compiler_params=pltpu.CompilerParams(
            dimension_semantics=("arbitrary",), vmem_limit_bytes=56 * 1024 * 1024
        ),
    )(*operands)


def exchange_in(pieces):
    stacked = jnp.transpose(jnp.concatenate(pieces, axis=-1), (1, 0, 2))
    moved = lax.all_to_all(stacked, "head", split_axis=0, concat_axis=0, tiled=True)
    return moved.reshape(moved.shape[0] * moved.shape[1], moved.shape[2])


def exchange_out(group_block, parts):
    shared = lax.axis_size("head")
    split = group_block.reshape(shared, group_block.shape[0] // shared, group_block.shape[1])
    moved = lax.all_to_all(split, "head", split_axis=0, concat_axis=0, tiled=True)
    return jnp.transpose(moved, (1, 0, 2))


def body(queries, keys, values, grad_out):
    token_count = queries.shape[0]
    shared = KVH
    group_size = QH // KVH
    query_rows = queries.reshape(token_count, shared, group_size, HD)
    grad_rows = grad_out.reshape(token_count, shared, group_size, HD)
    key_rows = keys.reshape(token_count, shared, HD)
    value_rows = values.reshape(token_count, shared, HD)
    first_part = exchange_in(
        [key_rows, value_rows, query_rows[:, :, 0], grad_rows[:, :, 0]]
    )
    second_part = exchange_in([query_rows[:, :, 1], grad_rows[:, :, 1]])
    group_rows = first_part.shape[0]
    first_query = lax.axis_index("ctx") * group_rows
    group_keys = first_part[:, :HD]
    group_values = first_part[:, HD : 2 * HD]
    key_tail, value_tail = shifted(
        (group_keys[group_rows - WIN :], group_values[group_rows - WIN :]), "ctx", 1
    )
    keys_ext = jnp.concatenate([key_tail, group_keys], axis=0)
    values_ext = jnp.concatenate([value_tail, group_values], axis=0)
    first_out, key_acc, value_acc = attend(first_part, 2, 3, keys_ext, values_ext, first_query)
    second_out, key_total, value_total = attend(
        second_part, 0, 1, keys_ext, values_ext, first_query, key_acc, value_acc
    )
    key_back, value_back = (
        shifted(key_total[:WIN].astype(jnp.bfloat16), "ctx", -1).astype(jnp.float32),
        shifted(value_total[:WIN].astype(jnp.bfloat16), "ctx", -1).astype(jnp.float32),
    )
    key_grad = jnp.concatenate(
        [key_total[WIN:group_rows], key_total[group_rows:] + key_back], axis=0
    ).astype(jnp.bfloat16)
    value_grad = jnp.concatenate(
        [value_total[WIN:group_rows], value_total[group_rows:] + value_back], axis=0
    ).astype(jnp.bfloat16)
    first_back = exchange_out(first_out, 2)
    second_back = exchange_out(jnp.concatenate([second_out, key_grad, value_grad], axis=1), 4)
    attended = jnp.stack([first_back[:, :, :HD], second_back[:, :, :HD]], axis=2)
    grad_queries = jnp.stack([first_back[:, :, HD:], second_back[:, :, HD : 2 * HD]], axis=2)
    return (
        attended.reshape(token_count, QH * HD),
        grad_queries.reshape(token_count, QH * HD),
        second_back[:, :, 2 * HD : 3 * HD].reshape(token_count, KVH * HD),
        second_back[:, :, 3 * HD :].reshape(token_count, KVH * HD),
    )


def solution(mesh):
    placed = (
        P(("ctx", "head"), None),
        P(("ctx", "head"), None),
        P(("ctx", "head"), None),
        P(("ctx", "head"), None),
    )
    return jax.shard_map(
        body,
        mesh=mesh,
        in_specs=placed,
        out_specs=(
            P(("ctx", "head"), None),
            P(("ctx", "head"), None),
            P(("ctx", "head"), None),
            P(("ctx", "head"), None),
        ),
        check_vma=False,
    )
```

```python
import functools

import jax
import jax.numpy as jnp
from jax import lax
from jax.experimental import pallas as pl
from jax.experimental.pallas import tpu as pltpu
from jax.sharding import PartitionSpec as P

HD = 128
QH = 32
KVH = 16
WIN = 1024
QPRE = 168
BLK = 256


def shifted(block, axis, distance):
    devices = range(lax.axis_size(axis))
    route = [(i - distance, i) for i in devices if i - distance in devices]
    return lax.ppermute(block, axis, route)


def attend_kernel(first_ref, q_ref, g_ref, k_ref, v_ref, *rest, block_offset, key_shift, carry):
    if carry:
        _, dk_in_ref, dv_in_ref, od_ref, dk_ref, dv_ref = rest
    else:
        od_ref, dk_ref, dv_ref = rest
    step = pl.program_id(0)
    block = step + block_offset
    rows = q_ref.shape[0]
    span = WIN + rows
    scale = QPRE ** (-0.5)

    @pl.when(step == 0)
    def _():
        if carry:
            dk_ref[...] = dk_in_ref[...]
            dv_ref[...] = dv_in_ref[...]
        else:
            dk_ref[...] = jnp.zeros_like(dk_ref)
            dv_ref[...] = jnp.zeros_like(dv_ref)

    start = pl.multiple_of(block * rows, rows)
    key_start = pl.multiple_of(block * rows - key_shift, rows)
    k_win = k_ref[pl.ds(key_start, span), :]
    v_win = v_ref[pl.ds(key_start, span), :]
    row_id = lax.broadcasted_iota(jnp.int32, (rows, span), 0)
    col_id = lax.broadcasted_iota(jnp.int32, (rows, span), 1)
    distance = row_id + WIN - col_id
    key_pos = first_ref[0] - WIN + start + col_id
    allowed = (distance >= 0) & (distance < WIN) & (key_pos >= 0)
    nt = (((1,), (1,)), ((), ()))
    tn = (((0,), (0,)), ((), ()))
    q = q_ref[...]
    g = g_ref[...]
    scores = lax.dot_general(q, k_win, nt, preferred_element_type=jnp.float32) * scale
    scores = jnp.where(allowed, scores, -jnp.inf)
    largest = jnp.max(scores, axis=-1, keepdims=True)
    unnormed = jnp.exp(scores - largest)
    probs = unnormed / jnp.sum(unnormed, axis=-1, keepdims=True)
    probs_low = probs.astype(jnp.bfloat16)
    out = jnp.dot(probs_low, v_win, preferred_element_type=jnp.float32).astype(jnp.bfloat16)
    od_ref[:, :HD] = out
    grad_probs = lax.dot_general(g, v_win, nt, preferred_element_type=jnp.float32)
    inner = jnp.sum(g.astype(jnp.float32) * out.astype(jnp.float32), axis=-1, keepdims=True)
    grad_scores = (probs * (grad_probs - inner) * scale).astype(jnp.bfloat16)
    od_ref[:, HD:] = jnp.dot(grad_scores, k_win, preferred_element_type=jnp.float32).astype(
        jnp.bfloat16
    )
    dk_ref[pl.ds(start, span), :] += lax.dot_general(
        grad_scores, q, tn, preferred_element_type=jnp.float32
    )
    dv_ref[pl.ds(start, span), :] += lax.dot_general(
        probs_low, g, tn, preferred_element_type=jnp.float32
    )


def attend(source, q_col, g_col, keys, values, first_query, blocks, key_shift, carried=None):
    query_count = source.shape[0]
    ext_rows = WIN + query_count
    rows = BLK
    block_offset, block_count = blocks
    first = jnp.reshape(first_query, (1,)).astype(jnp.int32)
    key_spec = pl.BlockSpec(keys.shape, lambda b, f: (0, 0))
    whole = pl.BlockSpec((ext_rows, HD), lambda b, f: (0, 0))
    in_specs = [
        pl.BlockSpec((rows, HD), lambda b, f: (b + block_offset, q_col)),
        pl.BlockSpec((rows, HD), lambda b, f: (b + block_offset, g_col)),
        key_spec,
        key_spec,
    ]
    operands = [first, source, source, keys, values]
    aliases = {}
    if carried is not None:
        in_specs += [pl.BlockSpec(memory_space=pl.ANY), whole, whole]
        operands += list(carried)
        aliases = {5: 0, 6: 1, 7: 2}
    grid_spec = pltpu.PrefetchScalarGridSpec(
        num_scalar_prefetch=1,
        grid=(block_count,),
        in_specs=in_specs,
        out_specs=[
            pl.BlockSpec((rows, 2 * HD), lambda b, f: (b + block_offset, 0)),
            whole,
            whole,
        ],
    )
    kernel = functools.partial(
        attend_kernel, block_offset=block_offset, key_shift=key_shift, carry=carried is not None
    )
    return pl.pallas_call(
        kernel,
        grid_spec=grid_spec,
        out_shape=[
            jax.ShapeDtypeStruct((query_count, 2 * HD), jnp.bfloat16),
            jax.ShapeDtypeStruct((ext_rows, HD), jnp.float32),
            jax.ShapeDtypeStruct((ext_rows, HD), jnp.float32),
        ],
        input_output_aliases=aliases,
        compiler_params=pltpu.CompilerParams(
            dimension_semantics=("arbitrary",), vmem_limit_bytes=56 * 1024 * 1024
        ),
    )(*operands)


def exchange_in(pieces):
    stacked = jnp.transpose(jnp.concatenate(pieces, axis=-1), (1, 0, 2))
    moved = lax.all_to_all(stacked, "head", split_axis=0, concat_axis=0, tiled=True)
    return moved.reshape(moved.shape[0] * moved.shape[1], moved.shape[2])


def exchange_out(group_block):
    shared = lax.axis_size("head")
    split = group_block.reshape(shared, group_block.shape[0] // shared, group_block.shape[1])
    moved = lax.all_to_all(split, "head", split_axis=0, concat_axis=0, tiled=True)
    return jnp.transpose(moved, (1, 0, 2))


def body(queries, keys, values, grad_out):
    token_count = queries.shape[0]
    shared = KVH
    pair = (QH // KVH) * HD
    query_rows = queries.reshape(token_count, shared, pair)
    grad_rows = grad_out.reshape(token_count, shared, pair)
    key_rows = keys.reshape(token_count, shared, HD)
    value_rows = values.reshape(token_count, shared, HD)
    first_part = exchange_in(
        [key_rows, value_rows, query_rows[:, :, :HD], grad_rows[:, :, :HD]]
    )
    second_part = exchange_in([query_rows[:, :, HD:], grad_rows[:, :, HD:]])
    group_rows = first_part.shape[0]
    block_total = group_rows // BLK
    lead = WIN // BLK
    first_query = lax.axis_index("ctx") * group_rows
    group_keys = first_part[:, :HD]
    group_values = first_part[:, HD : 2 * HD]
    key_tail, value_tail = shifted(
        (group_keys[group_rows - WIN :], group_values[group_rows - WIN :]), "ctx", 1
    )
    late = (lead, block_total - lead)
    early = (0, lead)
    carried = attend(first_part, 2, 3, group_keys, group_values, first_query, late, WIN)
    keys_ext = jnp.concatenate([key_tail, group_keys], axis=0)
    values_ext = jnp.concatenate([value_tail, group_values], axis=0)
    first_out, key_acc, value_acc = attend(
        first_part, 2, 3, keys_ext, values_ext, first_query, early, 0, carried
    )
    carried = attend(
        second_part, 0, 1, keys_ext, values_ext, first_query, early, 0,
        (jnp.zeros_like(first_out), key_acc, value_acc),
    )
    key_back, value_back = (
        shifted(carried[1][:WIN].astype(jnp.bfloat16), "ctx", -1).astype(jnp.float32),
        shifted(carried[2][:WIN].astype(jnp.bfloat16), "ctx", -1).astype(jnp.float32),
    )
    second_out, key_total, value_total = attend(
        second_part, 0, 1, keys_ext, values_ext, first_query, late, 0, carried
    )
    key_grad = jnp.concatenate(
        [key_total[WIN:group_rows], key_total[group_rows:] + key_back], axis=0
    ).astype(jnp.bfloat16)
    value_grad = jnp.concatenate(
        [value_total[WIN:group_rows], value_total[group_rows:] + value_back], axis=0
    ).astype(jnp.bfloat16)
    first_back = exchange_out(first_out)
    second_back = exchange_out(jnp.concatenate([second_out, key_grad, value_grad], axis=1))
    attended = jnp.concatenate([first_back[:, :, :HD], second_back[:, :, :HD]], axis=2)
    grad_queries = jnp.concatenate(
        [first_back[:, :, HD:], second_back[:, :, HD : 2 * HD]], axis=2
    )
    return (
        attended.reshape(token_count, QH * HD),
        grad_queries.reshape(token_count, QH * HD),
        second_back[:, :, 2 * HD : 3 * HD].reshape(token_count, KVH * HD),
        second_back[:, :, 3 * HD :].reshape(token_count, KVH * HD),
    )


def solution(mesh):
    placed = (
        P(("ctx", "head"), None),
        P(("ctx", "head"), None),
        P(("ctx", "head"), None),
        P(("ctx", "head"), None),
    )
    return jax.shard_map(
        body,
        mesh=mesh,
        in_specs=placed,
        out_specs=(
            P(("ctx", "head"), None),
            P(("ctx", "head"), None),
            P(("ctx", "head"), None),
            P(("ctx", "head"), None),
        ),
        check_vma=False,
    )
```

```python
import functools

import jax
import jax.numpy as jnp
from jax import lax
from jax.experimental import pallas as pl
from jax.experimental.pallas import tpu as pltpu
from jax.sharding import PartitionSpec as P

HD = 128
QH = 32
KVH = 16
WIN = 1024
QPRE = 168
BLK = 256


def shifted(block, axis, distance):
    devices = range(lax.axis_size(axis))
    route = [(i - distance, i) for i in devices if i - distance in devices]
    return lax.ppermute(block, axis, route)


def attend_kernel(first_ref, *refs, heads, block_offset, key_shift, carry):
    q_refs = refs[0 : 2 * heads : 2]
    g_refs = refs[1 : 2 * heads : 2]
    k_ref, v_ref = refs[2 * heads : 2 * heads + 2]
    rest = refs[2 * heads + 2 :]
    if carry:
        rest = rest[heads:]
        dk_in_ref, dv_in_ref = rest[:2]
        rest = rest[2:]
    od_refs = rest[:heads]
    dk_ref, dv_ref = rest[heads:]
    step = pl.program_id(0)
    block = step + block_offset
    rows = q_refs[0].shape[0]
    span = WIN + rows
    scale = QPRE ** (-0.5)

    @pl.when(step == 0)
    def _():
        if carry:
            dk_ref[...] = dk_in_ref[...]
            dv_ref[...] = dv_in_ref[...]
        else:
            dk_ref[...] = jnp.zeros_like(dk_ref)
            dv_ref[...] = jnp.zeros_like(dv_ref)

    start = pl.multiple_of(block * rows, rows)
    key_start = pl.multiple_of(block * rows - key_shift, rows)
    k_win = k_ref[pl.ds(key_start, span), :]
    v_win = v_ref[pl.ds(key_start, span), :]
    row_id = lax.broadcasted_iota(jnp.int32, (rows, span), 0)
    col_id = lax.broadcasted_iota(jnp.int32, (rows, span), 1)
    distance = row_id + WIN - col_id
    key_pos = first_ref[0] - WIN + start + col_id
    allowed = (distance >= 0) & (distance < WIN) & (key_pos >= 0)
    nt = (((1,), (1,)), ((), ()))
    tn = (((0,), (0,)), ((), ()))
    dk_acc = None
    dv_acc = None
    for q_ref, g_ref, od_ref in zip(q_refs, g_refs, od_refs):
        q = q_ref[...]
        g = g_ref[...]
        scores = lax.dot_general(q, k_win, nt, preferred_element_type=jnp.float32) * scale
        scores = jnp.where(allowed, scores, -jnp.inf)
        largest = jnp.max(scores, axis=-1, keepdims=True)
        unnormed = jnp.exp(scores - largest)
        probs = unnormed * (1.0 / jnp.sum(unnormed, axis=-1, keepdims=True))
        probs_low = probs.astype(jnp.bfloat16)
        out = jnp.dot(probs_low, v_win, preferred_element_type=jnp.float32).astype(jnp.bfloat16)
        od_ref[:, :HD] = out
        grad_probs = lax.dot_general(g, v_win, nt, preferred_element_type=jnp.float32)
        inner = jnp.sum(g.astype(jnp.float32) * out.astype(jnp.float32), axis=-1, keepdims=True)
        grad_scores = (probs * (grad_probs - inner) * scale).astype(jnp.bfloat16)
        od_ref[:, HD:] = jnp.dot(grad_scores, k_win, preferred_element_type=jnp.float32).astype(
            jnp.bfloat16
        )
        dk_part = lax.dot_general(grad_scores, q, tn, preferred_element_type=jnp.float32)
        dv_part = lax.dot_general(probs_low, g, tn, preferred_element_type=jnp.float32)
        dk_acc = dk_part if dk_acc is None else dk_acc + dk_part
        dv_acc = dv_part if dv_acc is None else dv_acc + dv_part
    dk_ref[pl.ds(start, span), :] += dk_acc
    dv_ref[pl.ds(start, span), :] += dv_acc


def attend(sources, keys, values, first_query, blocks, key_shift, carried=None):
    heads = len(sources)
    query_count = sources[0][0].shape[0]
    ext_rows = WIN + query_count
    rows = BLK
    block_offset, block_count = blocks
    first = jnp.reshape(first_query, (1,)).astype(jnp.int32)
    key_spec = pl.BlockSpec(keys.shape, lambda b, f: (0, 0))
    whole = pl.BlockSpec((ext_rows, HD), lambda b, f: (0, 0))
    in_specs = []
    operands = [first]
    for source, q_col, g_col in sources:
        in_specs += [
            pl.BlockSpec((rows, HD), lambda b, f, c=q_col: (b + block_offset, c)),
            pl.BlockSpec((rows, HD), lambda b, f, c=g_col: (b + block_offset, c)),
        ]
        operands += [source, source]
    in_specs += [key_spec, key_spec]
    operands += [keys, values]
    aliases = {}
    if carried is not None:
        base = len(operands)
        in_specs += [pl.BlockSpec(memory_space=pl.ANY)] * heads + [whole, whole]
        operands += list(carried)
        aliases = {base + i: i for i in range(heads + 2)}
    grid_spec = pltpu.PrefetchScalarGridSpec(
        num_scalar_prefetch=1,
        grid=(block_count,),
        in_specs=in_specs,
        out_specs=[pl.BlockSpec((rows, 2 * HD), lambda b, f: (b + block_offset, 0))] * heads
        + [whole, whole],
    )
    kernel = functools.partial(
        attend_kernel,
        heads=heads,
        block_offset=block_offset,
        key_shift=key_shift,
        carry=carried is not None,
    )
    return pl.pallas_call(
        kernel,
        grid_spec=grid_spec,
        out_shape=[jax.ShapeDtypeStruct((query_count, 2 * HD), jnp.bfloat16)] * heads
        + [
            jax.ShapeDtypeStruct((ext_rows, HD), jnp.float32),
            jax.ShapeDtypeStruct((ext_rows, HD), jnp.float32),
        ],
        input_output_aliases=aliases,
        compiler_params=pltpu.CompilerParams(
            dimension_semantics=("arbitrary",), vmem_limit_bytes=56 * 1024 * 1024
        ),
    )(*operands)


def exchange_in(pieces):
    stacked = jnp.transpose(jnp.concatenate(pieces, axis=-1), (1, 0, 2))
    moved = lax.all_to_all(stacked, "head", split_axis=0, concat_axis=0, tiled=True)
    return moved.reshape(moved.shape[0] * moved.shape[1], moved.shape[2])


def exchange_out(group_block):
    shared = lax.axis_size("head")
    split = group_block.reshape(shared, group_block.shape[0] // shared, group_block.shape[1])
    moved = lax.all_to_all(split, "head", split_axis=0, concat_axis=0, tiled=True)
    return jnp.transpose(moved, (1, 0, 2))


def body(queries, keys, values, grad_out):
    token_count = queries.shape[0]
    shared = KVH
    pair = (QH // KVH) * HD
    query_rows = queries.reshape(token_count, shared, pair)
    grad_rows = grad_out.reshape(token_count, shared, pair)
    key_rows = keys.reshape(token_count, shared, HD)
    value_rows = values.reshape(token_count, shared, HD)
    first_part = exchange_in(
        [key_rows, value_rows, query_rows[:, :, :HD], grad_rows[:, :, :HD]]
    )
    second_part = exchange_in([query_rows[:, :, HD:], grad_rows[:, :, HD:]])
    group_rows = first_part.shape[0]
    block_total = group_rows // BLK
    lead = WIN // BLK
    first_query = lax.axis_index("ctx") * group_rows
    group_keys = first_part[:, :HD]
    group_values = first_part[:, HD : 2 * HD]
    tail = shifted(first_part[group_rows - WIN :, : 2 * HD], "ctx", 1)
    late = (lead, block_total - lead)
    early = (0, lead)
    head0 = (first_part, 2, 3)
    head1 = (second_part, 0, 1)
    carried = attend([head0], group_keys, group_values, first_query, late, WIN)
    keys_ext = jnp.concatenate([tail[:, :HD], group_keys], axis=0)
    values_ext = jnp.concatenate([tail[:, HD:], group_values], axis=0)
    first_out, second_out, key_acc, value_acc = attend(
        [head0, head1], keys_ext, values_ext, first_query, early, 0,
        (carried[0], jnp.zeros_like(carried[0]), carried[1], carried[2]),
    )
    back = shifted(
        jnp.concatenate([key_acc[:WIN], value_acc[:WIN]], axis=1).astype(jnp.bfloat16), "ctx", -1
    ).astype(jnp.float32)
    second_out, key_total, value_total = attend(
        [head1], keys_ext, values_ext, first_query, late, 0, (second_out, key_acc, value_acc)
    )
    key_grad = jnp.concatenate(
        [key_total[WIN:group_rows], key_total[group_rows:] + back[:, :HD]], axis=0
    ).astype(jnp.bfloat16)
    value_grad = jnp.concatenate(
        [value_total[WIN:group_rows], value_total[group_rows:] + back[:, HD:]], axis=0
    ).astype(jnp.bfloat16)
    first_back = exchange_out(first_out)
    second_back = exchange_out(jnp.concatenate([second_out, key_grad, value_grad], axis=1))
    attended = jnp.concatenate([first_back[:, :, :HD], second_back[:, :, :HD]], axis=2)
    grad_queries = jnp.concatenate(
        [first_back[:, :, HD:], second_back[:, :, HD : 2 * HD]], axis=2
    )
    return (
        attended.reshape(token_count, QH * HD),
        grad_queries.reshape(token_count, QH * HD),
        second_back[:, :, 2 * HD : 3 * HD].reshape(token_count, KVH * HD),
        second_back[:, :, 3 * HD :].reshape(token_count, KVH * HD),
    )


def solution(mesh):
    placed = (
        P(("ctx", "head"), None),
        P(("ctx", "head"), None),
        P(("ctx", "head"), None),
        P(("ctx", "head"), None),
    )
    return jax.shard_map(
        body,
        mesh=mesh,
        in_specs=placed,
        out_specs=(
            P(("ctx", "head"), None),
            P(("ctx", "head"), None),
            P(("ctx", "head"), None),
            P(("ctx", "head"), None),
        ),
        check_vma=False,
    )
```

```python
import functools

import jax
import jax.numpy as jnp
from jax import lax
from jax.experimental import pallas as pl
from jax.experimental.pallas import tpu as pltpu
from jax.sharding import PartitionSpec as P

HD = 128
QH = 32
KVH = 16
WIN = 1024
QPRE = 168
BLK = 256


def shifted(block, axis, distance):
    devices = range(lax.axis_size(axis))
    route = [(i - distance, i) for i in devices if i - distance in devices]
    return lax.ppermute(block, axis, route)


def attend_kernel(first_ref, *refs, heads, block_offset, early, carry_od, carry_acc):
    pos = 0
    q_refs, g_refs = [], []
    for _ in range(heads):
        q_refs.append(refs[pos])
        g_refs.append(refs[pos + 1])
        pos += 2
    if early:
        kt_ref, vt_ref, kg_ref, vg_ref = refs[pos : pos + 4]
        pos += 4
    else:
        k_ref, v_ref = refs[pos : pos + 2]
        pos += 2
    pos += sum(carry_od)
    if carry_acc:
        dk_in_ref, dv_in_ref = refs[pos : pos + 2]
        pos += 2
    od_refs = refs[pos : pos + heads]
    pos += heads
    dk_ref, dv_ref, bias_ref = refs[pos : pos + 3]
    pos += 3
    if early:
        kx_ref, vx_ref = refs[pos : pos + 2]
    step = pl.program_id(0)
    block = step + block_offset
    rows = q_refs[0].shape[0]
    span = WIN + rows
    scale = QPRE ** (-0.5)

    @pl.when(step == 0)
    def _():
        if carry_acc:
            dk_ref[...] = dk_in_ref[...]
            dv_ref[...] = dv_in_ref[...]
        else:
            dk_ref[...] = jnp.zeros_like(dk_ref)
            dv_ref[...] = jnp.zeros_like(dv_ref)
        row_id = lax.broadcasted_iota(jnp.int32, (rows, span), 0)
        col_id = lax.broadcasted_iota(jnp.int32, (rows, span), 1)
        distance = row_id + WIN - col_id
        band = (distance >= 0) & (distance < WIN)
        bias_ref[...] = jnp.where(band, 0.0, -jnp.inf).astype(jnp.float32)
        if early:
            kx_ref[:WIN, :] = kt_ref[...]
            kx_ref[WIN:, :] = kg_ref[...]
            vx_ref[:WIN, :] = vt_ref[...]
            vx_ref[WIN:, :] = vg_ref[...]

    start = pl.multiple_of(block * rows, rows)
    if early:
        k_win = kx_ref[pl.ds(start, span), :]
        v_win = vx_ref[pl.ds(start, span), :]
        col_id = lax.broadcasted_iota(jnp.int32, (rows, span), 1)
        key_pos = first_ref[0] - WIN + start + col_id
        bias = jnp.where(key_pos >= 0, bias_ref[...], -jnp.inf)
    else:
        key_start = pl.multiple_of(start - WIN, rows)
        k_win = k_ref[pl.ds(key_start, span), :]
        v_win = v_ref[pl.ds(key_start, span), :]
        bias = bias_ref[...]
    nt = (((1,), (1,)), ((), ()))
    tn = (((0,), (0,)), ((), ()))
    dk_acc = None
    dv_acc = None
    for q_ref, g_ref, od_ref in zip(q_refs, g_refs, od_refs):
        q = q_ref[...]
        g = g_ref[...]
        scores = lax.dot_general(q, k_win, nt, preferred_element_type=jnp.float32) * scale
        scores = scores + bias
        largest = jnp.max(scores, axis=-1, keepdims=True)
        unnormed = jnp.exp(scores - largest)
        probs = unnormed * (1.0 / jnp.sum(unnormed, axis=-1, keepdims=True))
        probs_low = probs.astype(jnp.bfloat16)
        out = jnp.dot(probs_low, v_win, preferred_element_type=jnp.float32).astype(jnp.bfloat16)
        od_ref[:, :HD] = out
        grad_probs = lax.dot_general(g, v_win, nt, preferred_element_type=jnp.float32)
        inner = jnp.sum(g.astype(jnp.float32) * out.astype(jnp.float32), axis=-1, keepdims=True)
        grad_scores = (probs * (grad_probs - inner) * scale).astype(jnp.bfloat16)
        od_ref[:, HD:] = jnp.dot(grad_scores, k_win, preferred_element_type=jnp.float32).astype(
            jnp.bfloat16
        )
        dk_part = lax.dot_general(grad_scores, q, tn, preferred_element_type=jnp.float32)
        dv_part = lax.dot_general(probs_low, g, tn, preferred_element_type=jnp.float32)
        dk_acc = dk_part if dk_acc is None else dk_acc + dk_part
        dv_acc = dv_part if dv_acc is None else dv_acc + dv_part
    dk_ref[pl.ds(start, span), :] += dk_acc
    dv_ref[pl.ds(start, span), :] += dv_acc


def attend(sources, first_part, tail, first_query, blocks, carried_od, carried_acc):
    heads = len(sources)
    query_count = first_part.shape[0]
    ext_rows = WIN + query_count
    rows = BLK
    span = WIN + rows
    block_offset, block_count = blocks
    early = tail is not None
    first = jnp.reshape(first_query, (1,)).astype(jnp.int32)
    whole = pl.BlockSpec((ext_rows, HD), lambda b, f: (0, 0))
    in_specs = []
    operands = [first]
    for source, q_col, g_col in sources:
        in_specs += [
            pl.BlockSpec((rows, HD), lambda b, f, c=q_col: (b + block_offset, c)),
            pl.BlockSpec((rows, HD), lambda b, f, c=g_col: (b + block_offset, c)),
        ]
        operands += [source, source]
    if early:
        piece = (WIN, HD)
        in_specs += [
            pl.BlockSpec(piece, lambda b, f: (0, 0)),
            pl.BlockSpec(piece, lambda b, f: (0, 1)),
            pl.BlockSpec(piece, lambda b, f: (0, 0)),
            pl.BlockSpec(piece, lambda b, f: (0, 1)),
        ]
        operands += [tail, tail, first_part, first_part]
    else:
        in_specs += [
            pl.BlockSpec((query_count, HD), lambda b, f: (0, 0)),
            pl.BlockSpec((query_count, HD), lambda b, f: (0, 1)),
        ]
        operands += [first_part, first_part]
    aliases = {}
    carry_od = tuple(od is not None for od in carried_od)
    for i, od in enumerate(carried_od):
        if od is not None:
            aliases[len(operands)] = i
            in_specs.append(pl.BlockSpec(memory_space=pl.ANY))
            operands.append(od)
    if carried_acc is not None:
        aliases[len(operands)] = heads
        aliases[len(operands) + 1] = heads + 1
        in_specs += [whole, whole]
        operands += list(carried_acc)
    scratch = [pltpu.VMEM((rows, span), jnp.float32)]
    if early:
        scratch += [pltpu.VMEM((2 * WIN, HD), jnp.bfloat16)] * 2
    grid_spec = pltpu.PrefetchScalarGridSpec(
        num_scalar_prefetch=1,
        grid=(block_count,),
        in_specs=in_specs,
        out_specs=[pl.BlockSpec((rows, 2 * HD), lambda b, f: (b + block_offset, 0))] * heads
        + [whole, whole],
        scratch_shapes=scratch,
    )
    kernel = functools.partial(
        attend_kernel,
        heads=heads,
        block_offset=block_offset,
        early=early,
        carry_od=carry_od,
        carry_acc=carried_acc is not None,
    )
    return pl.pallas_call(
        kernel,
        grid_spec=grid_spec,
        out_shape=[jax.ShapeDtypeStruct((query_count, 2 * HD), jnp.bfloat16)] * heads
        + [
            jax.ShapeDtypeStruct((ext_rows, HD), jnp.float32),
            jax.ShapeDtypeStruct((ext_rows, HD), jnp.float32),
        ],
        input_output_aliases=aliases,
        compiler_params=pltpu.CompilerParams(
            dimension_semantics=("arbitrary",), vmem_limit_bytes=56 * 1024 * 1024
        ),
    )(*operands)


def exchange_in(pieces):
    stacked = jnp.transpose(jnp.concatenate(pieces, axis=-1), (1, 0, 2))
    moved = lax.all_to_all(stacked, "head", split_axis=0, concat_axis=0, tiled=True)
    return moved.reshape(moved.shape[0] * moved.shape[1], moved.shape[2])


def exchange_out(group_block):
    shared = lax.axis_size("head")
    split = group_block.reshape(shared, group_block.shape[0] // shared, group_block.shape[1])
    moved = lax.all_to_all(split, "head", split_axis=0, concat_axis=0, tiled=True)
    return jnp.transpose(moved, (1, 0, 2))


def body(queries, keys, values, grad_out):
    token_count = queries.shape[0]
    shared = KVH
    pair = (QH // KVH) * HD
    query_rows = queries.reshape(token_count, shared, pair)
    grad_rows = grad_out.reshape(token_count, shared, pair)
    key_rows = keys.reshape(token_count, shared, HD)
    value_rows = values.reshape(token_count, shared, HD)
    first_part = exchange_in(
        [key_rows, value_rows, query_rows[:, :, :HD], grad_rows[:, :, :HD]]
    )
    second_part = exchange_in([query_rows[:, :, HD:], grad_rows[:, :, HD:]])
    group_rows = first_part.shape[0]
    block_total = group_rows // BLK
    lead = WIN // BLK
    first_query = lax.axis_index("ctx") * group_rows
    tail = shifted(first_part[group_rows - WIN :, : 2 * HD], "ctx", 1)
    late = (lead, block_total - lead)
    early = (0, lead)
    head0 = (first_part, 2, 3)
    head1 = (second_part, 0, 1)
    first_out, key_acc, value_acc = attend(
        [head0], first_part, None, first_query, late, (None,), None
    )
    first_out, second_out, key_acc, value_acc = attend(
        [head0, head1], first_part, tail, first_query, early, (first_out, None),
        (key_acc, value_acc),
    )
    back = shifted(
        jnp.concatenate([key_acc[:WIN], value_acc[:WIN]], axis=1).astype(jnp.bfloat16), "ctx", -1
    ).astype(jnp.float32)
    second_out, key_total, value_total = attend(
        [head1], first_part, None, first_query, late, (second_out,), (key_acc, value_acc)
    )
    first_back = exchange_out(first_out)
    second_back = exchange_out(second_out)
    key_grad = jnp.concatenate(
        [key_total[WIN:group_rows], key_total[group_rows:] + back[:, :HD]], axis=0
    ).astype(jnp.bfloat16)
    value_grad = jnp.concatenate(
        [value_total[WIN:group_rows], value_total[group_rows:] + back[:, HD:]], axis=0
    ).astype(jnp.bfloat16)
    grads_back = exchange_out(jnp.concatenate([key_grad, value_grad], axis=1))
    attended = jnp.concatenate([first_back[:, :, :HD], second_back[:, :, :HD]], axis=2)
    grad_queries = jnp.concatenate([first_back[:, :, HD:], second_back[:, :, HD:]], axis=2)
    return (
        attended.reshape(token_count, QH * HD),
        grad_queries.reshape(token_count, QH * HD),
        grads_back[:, :, :HD].reshape(token_count, KVH * HD),
        grads_back[:, :, HD:].reshape(token_count, KVH * HD),
    )


def solution(mesh):
    placed = (
        P(("ctx", "head"), None),
        P(("ctx", "head"), None),
        P(("ctx", "head"), None),
        P(("ctx", "head"), None),
    )
    return jax.shard_map(
        body,
        mesh=mesh,
        in_specs=placed,
        out_specs=(
            P(("ctx", "head"), None),
            P(("ctx", "head"), None),
            P(("ctx", "head"), None),
            P(("ctx", "head"), None),
        ),
        check_vma=False,
    )
```

```python
import functools

import jax
import jax.numpy as jnp
from jax import lax
from jax.experimental import pallas as pl
from jax.experimental.pallas import tpu as pltpu
from jax.sharding import PartitionSpec as P

HD = 128
QH = 32
KVH = 16
WIN = 1024
QPRE = 168
BLK = 256


def shifted(block, axis, distance):
    devices = range(lax.axis_size(axis))
    route = [(i - distance, i) for i in devices if i - distance in devices]
    return lax.ppermute(block, axis, route)


def attend_kernel(first_ref, *refs, heads, block_offset, early, carry_od, acc_base):
    pos = 0
    q_refs, g_refs = [], []
    for _ in range(heads):
        q_refs.append(refs[pos])
        g_refs.append(refs[pos + 1])
        pos += 2
    if early:
        kt_ref, vt_ref, kg_ref, vg_ref = refs[pos : pos + 4]
        pos += 4
    else:
        k_ref, v_ref = refs[pos : pos + 2]
        pos += 2
    pos += sum(carry_od)
    od_refs = refs[pos : pos + heads]
    pos += heads
    dk_ref, dv_ref, bias_ref = refs[pos : pos + 3]
    pos += 3
    if early:
        kx_ref, vx_ref = refs[pos : pos + 2]
    step = pl.program_id(0)
    block = step + block_offset
    rows = q_refs[0].shape[0]
    span = WIN + rows
    scale = QPRE ** (-0.5)

    @pl.when(step == 0)
    def _():
        dk_ref[...] = jnp.zeros_like(dk_ref)
        dv_ref[...] = jnp.zeros_like(dv_ref)
        row_id = lax.broadcasted_iota(jnp.int32, (rows, span), 0)
        col_id = lax.broadcasted_iota(jnp.int32, (rows, span), 1)
        distance = row_id + WIN - col_id
        band = (distance >= 0) & (distance < WIN)
        bias_ref[...] = jnp.where(band, 0.0, -jnp.inf).astype(jnp.float32)
        if early:
            kx_ref[:WIN, :] = kt_ref[...]
            kx_ref[WIN:, :] = kg_ref[...]
            vx_ref[:WIN, :] = vt_ref[...]
            vx_ref[WIN:, :] = vg_ref[...]

    start = pl.multiple_of(block * rows, rows)
    if early:
        k_win = kx_ref[pl.ds(start, span), :]
        v_win = vx_ref[pl.ds(start, span), :]
        col_id = lax.broadcasted_iota(jnp.int32, (rows, span), 1)
        key_pos = first_ref[0] - WIN + start + col_id
        bias = jnp.where(key_pos >= 0, bias_ref[...], -jnp.inf)
    else:
        key_start = pl.multiple_of(start - WIN, rows)
        k_win = k_ref[pl.ds(key_start, span), :]
        v_win = v_ref[pl.ds(key_start, span), :]
        bias = bias_ref[...]
    nt = (((1,), (1,)), ((), ()))
    tn = (((0,), (0,)), ((), ()))
    dk_acc = None
    dv_acc = None
    for q_ref, g_ref, od_ref in zip(q_refs, g_refs, od_refs):
        q = q_ref[...]
        g = g_ref[...]
        scores = lax.dot_general(q, k_win, nt, preferred_element_type=jnp.float32) * scale
        scores = scores + bias
        largest = jnp.max(scores, axis=-1, keepdims=True)
        unnormed = jnp.exp(scores - largest)
        probs = unnormed * (1.0 / jnp.sum(unnormed, axis=-1, keepdims=True))
        probs_low = probs.astype(jnp.bfloat16)
        out = jnp.dot(probs_low, v_win, preferred_element_type=jnp.float32).astype(jnp.bfloat16)
        od_ref[:, :HD] = out
        grad_probs = lax.dot_general(g, v_win, nt, preferred_element_type=jnp.float32)
        inner = jnp.sum(g.astype(jnp.float32) * out.astype(jnp.float32), axis=-1, keepdims=True)
        grad_scores = (probs * (grad_probs - inner) * scale).astype(jnp.bfloat16)
        od_ref[:, HD:] = jnp.dot(grad_scores, k_win, preferred_element_type=jnp.float32).astype(
            jnp.bfloat16
        )
        dk_part = lax.dot_general(grad_scores, q, tn, preferred_element_type=jnp.float32)
        dv_part = lax.dot_general(probs_low, g, tn, preferred_element_type=jnp.float32)
        dk_acc = dk_part if dk_acc is None else dk_acc + dk_part
        dv_acc = dv_part if dv_acc is None else dv_acc + dv_part
    acc_start = pl.multiple_of(start - acc_base, rows)
    dk_ref[pl.ds(acc_start, span), :] += dk_acc
    dv_ref[pl.ds(acc_start, span), :] += dv_acc


def attend(sources, first_part, tail, first_query, blocks, carried_od):
    heads = len(sources)
    query_count = first_part.shape[0]
    acc_base = 0 if tail is not None else WIN
    acc_rows = 2 * WIN if tail is not None else query_count
    rows = BLK
    span = WIN + rows
    block_offset, block_count = blocks
    early = tail is not None
    first = jnp.reshape(first_query, (1,)).astype(jnp.int32)
    whole = pl.BlockSpec((acc_rows, HD), lambda b, f: (0, 0))
    in_specs = []
    operands = [first]
    for source, q_col, g_col in sources:
        in_specs += [
            pl.BlockSpec((rows, HD), lambda b, f, c=q_col: (b + block_offset, c)),
            pl.BlockSpec((rows, HD), lambda b, f, c=g_col: (b + block_offset, c)),
        ]
        operands += [source, source]
    if early:
        piece = (WIN, HD)
        in_specs += [
            pl.BlockSpec(piece, lambda b, f: (0, 0)),
            pl.BlockSpec(piece, lambda b, f: (0, 1)),
            pl.BlockSpec(piece, lambda b, f: (0, 0)),
            pl.BlockSpec(piece, lambda b, f: (0, 1)),
        ]
        operands += [tail, tail, first_part, first_part]
    else:
        in_specs += [
            pl.BlockSpec((query_count, HD), lambda b, f: (0, 0)),
            pl.BlockSpec((query_count, HD), lambda b, f: (0, 1)),
        ]
        operands += [first_part, first_part]
    aliases = {}
    carry_od = tuple(od is not None for od in carried_od)
    for i, od in enumerate(carried_od):
        if od is not None:
            aliases[len(operands)] = i
            in_specs.append(pl.BlockSpec(memory_space=pl.ANY))
            operands.append(od)
    scratch = [pltpu.VMEM((rows, span), jnp.float32)]
    if early:
        scratch += [pltpu.VMEM((2 * WIN, HD), jnp.bfloat16)] * 2
    grid_spec = pltpu.PrefetchScalarGridSpec(
        num_scalar_prefetch=1,
        grid=(block_count,),
        in_specs=in_specs,
        out_specs=[pl.BlockSpec((rows, 2 * HD), lambda b, f: (b + block_offset, 0))] * heads
        + [whole, whole],
        scratch_shapes=scratch,
    )
    kernel = functools.partial(
        attend_kernel,
        heads=heads,
        block_offset=block_offset,
        early=early,
        carry_od=carry_od,
        acc_base=acc_base,
    )
    return pl.pallas_call(
        kernel,
        grid_spec=grid_spec,
        out_shape=[jax.ShapeDtypeStruct((query_count, 2 * HD), jnp.bfloat16)] * heads
        + [
            jax.ShapeDtypeStruct((acc_rows, HD), jnp.float32),
            jax.ShapeDtypeStruct((acc_rows, HD), jnp.float32),
        ],
        input_output_aliases=aliases,
        compiler_params=pltpu.CompilerParams(
            dimension_semantics=("arbitrary",), vmem_limit_bytes=56 * 1024 * 1024
        ),
    )(*operands)


def exchange_in(pieces):
    stacked = jnp.transpose(jnp.concatenate(pieces, axis=-1), (1, 0, 2))
    moved = lax.all_to_all(stacked, "head", split_axis=0, concat_axis=0, tiled=True)
    return moved.reshape(moved.shape[0] * moved.shape[1], moved.shape[2])


def exchange_out(group_block):
    shared = lax.axis_size("head")
    split = group_block.reshape(shared, group_block.shape[0] // shared, group_block.shape[1])
    moved = lax.all_to_all(split, "head", split_axis=0, concat_axis=0, tiled=True)
    return jnp.transpose(moved, (1, 0, 2))


def body(queries, keys, values, grad_out):
    token_count = queries.shape[0]
    shared = KVH
    pair = (QH // KVH) * HD
    query_rows = queries.reshape(token_count, shared, pair)
    grad_rows = grad_out.reshape(token_count, shared, pair)
    key_rows = keys.reshape(token_count, shared, HD)
    value_rows = values.reshape(token_count, shared, HD)
    first_part = exchange_in(
        [key_rows, value_rows, query_rows[:, :, :HD], grad_rows[:, :, :HD]]
    )
    second_part = exchange_in([query_rows[:, :, HD:], grad_rows[:, :, HD:]])
    group_rows = first_part.shape[0]
    block_total = group_rows // BLK
    lead = WIN // BLK
    first_query = lax.axis_index("ctx") * group_rows
    tail = shifted(first_part[group_rows - WIN :, : 2 * HD], "ctx", 1)
    late = (lead, block_total - lead)
    early = (0, lead)
    head0 = (first_part, 2, 3)
    head1 = (second_part, 0, 1)
    first_out, key_late, value_late = attend([head0], first_part, None, first_query, late, (None,))
    first_out, second_out, key_early, value_early = attend(
        [head0, head1], first_part, tail, first_query, early, (first_out, None)
    )
    back = shifted(
        jnp.concatenate([key_early[:WIN], value_early[:WIN]], axis=1).astype(jnp.bfloat16),
        "ctx",
        -1,
    ).astype(jnp.float32)
    second_out, key_last, value_last = attend(
        [head1], first_part, None, first_query, late, (second_out,)
    )
    first_back = exchange_out(first_out)
    second_back = exchange_out(second_out)
    lead_pad = ((0, group_rows - WIN), (0, 0))
    tail_pad = ((group_rows - WIN, 0), (0, 0))
    key_grad = (
        key_late + key_last + jnp.pad(key_early[WIN:], lead_pad) + jnp.pad(back[:, :HD], tail_pad)
    ).astype(jnp.bfloat16)
    value_grad = (
        value_late
        + value_last
        + jnp.pad(value_early[WIN:], lead_pad)
        + jnp.pad(back[:, HD:], tail_pad)
    ).astype(jnp.bfloat16)
    grads_back = exchange_out(jnp.concatenate([key_grad, value_grad], axis=1))
    attended = jnp.concatenate([first_back[:, :, :HD], second_back[:, :, :HD]], axis=2)
    grad_queries = jnp.concatenate([first_back[:, :, HD:], second_back[:, :, HD:]], axis=2)
    return (
        attended.reshape(token_count, QH * HD),
        grad_queries.reshape(token_count, QH * HD),
        grads_back[:, :, :HD].reshape(token_count, KVH * HD),
        grads_back[:, :, HD:].reshape(token_count, KVH * HD),
    )


def solution(mesh):
    placed = (
        P(("ctx", "head"), None),
        P(("ctx", "head"), None),
        P(("ctx", "head"), None),
        P(("ctx", "head"), None),
    )
    return jax.shard_map(
        body,
        mesh=mesh,
        in_specs=placed,
        out_specs=(
            P(("ctx", "head"), None),
            P(("ctx", "head"), None),
            P(("ctx", "head"), None),
            P(("ctx", "head"), None),
        ),
        check_vma=False,
    )
```

```python
import functools

import jax
import jax.numpy as jnp
from jax import lax
from jax.experimental import pallas as pl
from jax.experimental.pallas import tpu as pltpu
from jax.sharding import PartitionSpec as P

HD = 128
QH = 32
KVH = 16
WIN = 1024
QPRE = 168
BLK = 256


def shifted(block, axis, distance):
    devices = range(lax.axis_size(axis))
    route = [(i - distance, i) for i in devices if i - distance in devices]
    return lax.ppermute(block, axis, route)


def attend_kernel(first_ref, *refs, heads, block_offset, early, carry_od, acc_base):
    pos = 0
    q_refs, g_refs = [], []
    for _ in range(heads):
        q_refs.append(refs[pos])
        g_refs.append(refs[pos + 1])
        pos += 2
    if early:
        kt_ref, vt_ref, kg_ref, vg_ref = refs[pos : pos + 4]
        pos += 4
    else:
        k_ref, v_ref = refs[pos : pos + 2]
        pos += 2
    pos += sum(carry_od)
    od_refs = refs[pos : pos + heads]
    pos += heads
    dk_ref, dv_ref, bias_ref = refs[pos : pos + 3]
    pos += 3
    if early:
        kx_ref, vx_ref = refs[pos : pos + 2]
    step = pl.program_id(0)
    block = step + block_offset
    rows = q_refs[0].shape[0]
    span = WIN + rows
    scale = QPRE ** (-0.5)

    @pl.when(step == 0)
    def _():
        dk_ref[...] = jnp.zeros_like(dk_ref)
        dv_ref[...] = jnp.zeros_like(dv_ref)
        row_id = lax.broadcasted_iota(jnp.int32, (rows, span), 0)
        col_id = lax.broadcasted_iota(jnp.int32, (rows, span), 1)
        distance = row_id + WIN - col_id
        band = (distance >= 0) & (distance < WIN)
        bias_ref[...] = jnp.where(band, 0.0, -jnp.inf).astype(jnp.float32)
        if early:
            kx_ref[:WIN, :] = kt_ref[...]
            kx_ref[WIN:, :] = kg_ref[...]
            vx_ref[:WIN, :] = vt_ref[...]
            vx_ref[WIN:, :] = vg_ref[...]

    start = pl.multiple_of(block * rows, rows)
    if early:
        k_win = kx_ref[pl.ds(start, span), :]
        v_win = vx_ref[pl.ds(start, span), :]
        col_id = lax.broadcasted_iota(jnp.int32, (rows, span), 1)
        key_pos = first_ref[0] - WIN + start + col_id
        bias = jnp.where(key_pos >= 0, bias_ref[...], -jnp.inf)
    else:
        key_start = pl.multiple_of(start - WIN, rows)
        k_win = k_ref[pl.ds(key_start, span), :]
        v_win = v_ref[pl.ds(key_start, span), :]
        bias = bias_ref[...]
    nt = (((1,), (1,)), ((), ()))
    tn = (((0,), (0,)), ((), ()))
    dk_acc = None
    dv_acc = None
    for q_ref, g_ref, od_ref in zip(q_refs, g_refs, od_refs):
        q = q_ref[...]
        g = g_ref[...]
        scores = lax.dot_general(q, k_win, nt, preferred_element_type=jnp.float32) * scale
        scores = scores + bias
        largest = jnp.max(scores, axis=-1, keepdims=True)
        unnormed = jnp.exp(scores - largest)
        probs = unnormed * (1.0 / jnp.sum(unnormed, axis=-1, keepdims=True))
        probs_low = probs.astype(jnp.bfloat16)
        out = jnp.dot(probs_low, v_win, preferred_element_type=jnp.float32).astype(jnp.bfloat16)
        od_ref[:, :HD] = out
        grad_probs = lax.dot_general(g, v_win, nt, preferred_element_type=jnp.float32)
        inner = jnp.sum(g.astype(jnp.float32) * out.astype(jnp.float32), axis=-1, keepdims=True)
        grad_scores = (probs * (grad_probs - inner) * scale).astype(jnp.bfloat16)
        od_ref[:, HD:] = jnp.dot(grad_scores, k_win, preferred_element_type=jnp.float32).astype(
            jnp.bfloat16
        )
        dk_part = lax.dot_general(grad_scores, q, tn, preferred_element_type=jnp.float32)
        dv_part = lax.dot_general(probs_low, g, tn, preferred_element_type=jnp.float32)
        dk_acc = dk_part if dk_acc is None else dk_acc + dk_part
        dv_acc = dv_part if dv_acc is None else dv_acc + dv_part
    acc_start = pl.multiple_of(start - acc_base, rows)
    dk_ref[pl.ds(acc_start, span), :] += dk_acc
    dv_ref[pl.ds(acc_start, span), :] += dv_acc


def attend(sources, first_part, tail, first_query, blocks, carried_od):
    heads = len(sources)
    query_count = first_part.shape[0]
    acc_base = 0 if tail is not None else WIN
    acc_rows = 2 * WIN if tail is not None else query_count
    rows = BLK
    span = WIN + rows
    block_offset, block_count = blocks
    early = tail is not None
    first = jnp.reshape(first_query, (1,)).astype(jnp.int32)
    whole = pl.BlockSpec((acc_rows, HD), lambda b, f: (0, 0))
    in_specs = []
    operands = [first]
    for source, q_col, g_col in sources:
        in_specs += [
            pl.BlockSpec((rows, HD), lambda b, f, c=q_col: (b + block_offset, c)),
            pl.BlockSpec((rows, HD), lambda b, f, c=g_col: (b + block_offset, c)),
        ]
        operands += [source, source]
    if early:
        piece = (WIN, HD)
        in_specs += [
            pl.BlockSpec(piece, lambda b, f: (0, 0)),
            pl.BlockSpec(piece, lambda b, f: (0, 1)),
            pl.BlockSpec(piece, lambda b, f: (0, 0)),
            pl.BlockSpec(piece, lambda b, f: (0, 1)),
        ]
        operands += [tail, tail, first_part, first_part]
    else:
        in_specs += [
            pl.BlockSpec((query_count, HD), lambda b, f: (0, 0)),
            pl.BlockSpec((query_count, HD), lambda b, f: (0, 1)),
        ]
        operands += [first_part, first_part]
    aliases = {}
    carry_od = tuple(od is not None for od in carried_od)
    for i, od in enumerate(carried_od):
        if od is not None:
            aliases[len(operands)] = i
            in_specs.append(pl.BlockSpec(memory_space=pl.ANY))
            operands.append(od)
    scratch = [pltpu.VMEM((rows, span), jnp.float32)]
    if early:
        scratch += [pltpu.VMEM((2 * WIN, HD), jnp.bfloat16)] * 2
    grid_spec = pltpu.PrefetchScalarGridSpec(
        num_scalar_prefetch=1,
        grid=(block_count,),
        in_specs=in_specs,
        out_specs=[pl.BlockSpec((rows, 2 * HD), lambda b, f: (b + block_offset, 0))] * heads
        + [whole, whole],
        scratch_shapes=scratch,
    )
    kernel = functools.partial(
        attend_kernel,
        heads=heads,
        block_offset=block_offset,
        early=early,
        carry_od=carry_od,
        acc_base=acc_base,
    )
    return pl.pallas_call(
        kernel,
        grid_spec=grid_spec,
        out_shape=[jax.ShapeDtypeStruct((query_count, 2 * HD), jnp.bfloat16)] * heads
        + [
            jax.ShapeDtypeStruct((acc_rows, HD), jnp.float32),
            jax.ShapeDtypeStruct((acc_rows, HD), jnp.float32),
        ],
        input_output_aliases=aliases,
        compiler_params=pltpu.CompilerParams(
            dimension_semantics=("arbitrary",), vmem_limit_bytes=56 * 1024 * 1024
        ),
    )(*operands)


def exchange_in(pieces):
    stacked = jnp.transpose(jnp.concatenate(pieces, axis=-1), (1, 0, 2))
    moved = lax.all_to_all(stacked, "head", split_axis=0, concat_axis=0, tiled=True)
    return moved.reshape(moved.shape[0] * moved.shape[1], moved.shape[2])


def exchange_out(group_block):
    shared = lax.axis_size("head")
    split = group_block.reshape(shared, group_block.shape[0] // shared, group_block.shape[1])
    moved = lax.all_to_all(split, "head", split_axis=0, concat_axis=0, tiled=True)
    return jnp.transpose(moved, (1, 0, 2))


def body(queries, keys, values, grad_out):
    token_count = queries.shape[0]
    shared = KVH
    pair = (QH // KVH) * HD
    query_rows = queries.reshape(token_count, shared, pair)
    grad_rows = grad_out.reshape(token_count, shared, pair)
    key_rows = keys.reshape(token_count, shared, HD)
    value_rows = values.reshape(token_count, shared, HD)
    first_part = exchange_in([key_rows, value_rows])
    head0_part = exchange_in([query_rows[:, :, :HD], grad_rows[:, :, :HD]])
    second_part = exchange_in([query_rows[:, :, HD:], grad_rows[:, :, HD:]])
    group_rows = first_part.shape[0]
    block_total = group_rows // BLK
    lead = WIN // BLK
    first_query = lax.axis_index("ctx") * group_rows
    tail = shifted(first_part[group_rows - WIN :], "ctx", 1)
    late = (lead, block_total - lead)
    early = (0, lead)
    head0 = (head0_part, 0, 1)
    head1 = (second_part, 0, 1)
    first_out, key_late, value_late = attend([head0], first_part, None, first_query, late, (None,))
    first_out, second_out, key_early, value_early = attend(
        [head0, head1], first_part, tail, first_query, early, (first_out, None)
    )
    back = shifted(
        jnp.concatenate([key_early[:WIN], value_early[:WIN]], axis=1).astype(jnp.bfloat16),
        "ctx",
        -1,
    ).astype(jnp.float32)
    second_out, key_last, value_last = attend(
        [head1], first_part, None, first_query, late, (second_out,)
    )
    first_back = exchange_out(first_out)
    second_back = exchange_out(second_out)
    lead_pad = ((0, group_rows - WIN), (0, 0))
    tail_pad = ((group_rows - WIN, 0), (0, 0))
    key_grad = (
        key_late + key_last + jnp.pad(key_early[WIN:], lead_pad) + jnp.pad(back[:, :HD], tail_pad)
    ).astype(jnp.bfloat16)
    value_grad = (
        value_late
        + value_last
        + jnp.pad(value_early[WIN:], lead_pad)
        + jnp.pad(back[:, HD:], tail_pad)
    ).astype(jnp.bfloat16)
    grads_back = exchange_out(jnp.concatenate([key_grad, value_grad], axis=1))
    attended = jnp.concatenate([first_back[:, :, :HD], second_back[:, :, :HD]], axis=2)
    grad_queries = jnp.concatenate([first_back[:, :, HD:], second_back[:, :, HD:]], axis=2)
    return (
        attended.reshape(token_count, QH * HD),
        grad_queries.reshape(token_count, QH * HD),
        grads_back[:, :, :HD].reshape(token_count, KVH * HD),
        grads_back[:, :, HD:].reshape(token_count, KVH * HD),
    )


def solution(mesh):
    placed = (
        P(("ctx", "head"), None),
        P(("ctx", "head"), None),
        P(("ctx", "head"), None),
        P(("ctx", "head"), None),
    )
    return jax.shard_map(
        body,
        mesh=mesh,
        in_specs=placed,
        out_specs=(
            P(("ctx", "head"), None),
            P(("ctx", "head"), None),
            P(("ctx", "head"), None),
            P(("ctx", "head"), None),
        ),
        check_vma=False,
    )
```

```python
import functools

import jax
import jax.numpy as jnp
from jax import lax
from jax.experimental import pallas as pl
from jax.experimental.pallas import tpu as pltpu
from jax.sharding import PartitionSpec as P

HD = 128
QH = 32
KVH = 16
WIN = 1024
QPRE = 168
BLK = 256


def shifted(block, axis, distance):
    devices = range(lax.axis_size(axis))
    route = [(i - distance, i) for i in devices if i - distance in devices]
    return lax.ppermute(block, axis, route)


def attend_kernel(first_ref, *refs, heads, block_offset, early, carry_od, acc_base):
    pos = 0
    q_refs, g_refs = [], []
    for _ in range(heads):
        q_refs.append(refs[pos])
        g_refs.append(refs[pos + 1])
        pos += 2
    if early:
        kt_ref, vt_ref, kg_ref, vg_ref = refs[pos : pos + 4]
        pos += 4
    else:
        k_ref, v_ref = refs[pos : pos + 2]
        pos += 2
    pos += sum(carry_od)
    od_refs = refs[pos : pos + heads]
    pos += heads
    dk_ref, dv_ref = refs[pos : pos + 2]
    pos += 2
    if early:
        halo_ref = refs[pos]
        pos += 1
    bias_ref = refs[pos]
    pos += 1
    if early:
        kx_ref, vx_ref = refs[pos : pos + 2]
    step = pl.program_id(0)
    block = step + block_offset
    rows = q_refs[0].shape[0]
    span = WIN + rows
    scale = QPRE ** (-0.5)

    @pl.when(step == 0)
    def _():
        dk_ref[...] = jnp.zeros_like(dk_ref)
        dv_ref[...] = jnp.zeros_like(dv_ref)
        row_id = lax.broadcasted_iota(jnp.int32, (rows, span), 0)
        col_id = lax.broadcasted_iota(jnp.int32, (rows, span), 1)
        distance = row_id + WIN - col_id
        band = (distance >= 0) & (distance < WIN)
        bias_ref[...] = jnp.where(band, 0.0, -jnp.inf).astype(jnp.float32)
        if early:
            kx_ref[:WIN, :] = kt_ref[...]
            kx_ref[WIN:, :] = kg_ref[...]
            vx_ref[:WIN, :] = vt_ref[...]
            vx_ref[WIN:, :] = vg_ref[...]

    start = pl.multiple_of(block * rows, rows)
    if early:
        k_win = kx_ref[pl.ds(start, span), :]
        v_win = vx_ref[pl.ds(start, span), :]
        col_id = lax.broadcasted_iota(jnp.int32, (rows, span), 1)
        key_pos = first_ref[0] - WIN + start + col_id
        bias = jnp.where(key_pos >= 0, bias_ref[...], -jnp.inf)
    else:
        key_start = pl.multiple_of(start - WIN, rows)
        k_win = k_ref[pl.ds(key_start, span), :]
        v_win = v_ref[pl.ds(key_start, span), :]
        bias = bias_ref[...]
    nt = (((1,), (1,)), ((), ()))
    tn = (((0,), (0,)), ((), ()))
    dk_acc = None
    dv_acc = None
    for q_ref, g_ref, od_ref in zip(q_refs, g_refs, od_refs):
        q = q_ref[...]
        g = g_ref[...]
        scores = lax.dot_general(q, k_win, nt, preferred_element_type=jnp.float32) * scale
        scores = scores + bias
        largest = jnp.max(scores, axis=-1, keepdims=True)
        unnormed = jnp.exp(scores - largest)
        probs = unnormed * (1.0 / jnp.sum(unnormed, axis=-1, keepdims=True))
        probs_low = probs.astype(jnp.bfloat16)
        out = jnp.dot(probs_low, v_win, preferred_element_type=jnp.float32).astype(jnp.bfloat16)
        od_ref[:, :HD] = out
        grad_probs = lax.dot_general(g, v_win, nt, preferred_element_type=jnp.float32)
        inner = jnp.sum(g.astype(jnp.float32) * out.astype(jnp.float32), axis=-1, keepdims=True)
        grad_scores = (probs * (grad_probs - inner) * scale).astype(jnp.bfloat16)
        od_ref[:, HD:] = jnp.dot(grad_scores, k_win, preferred_element_type=jnp.float32).astype(
            jnp.bfloat16
        )
        dk_part = lax.dot_general(grad_scores, q, tn, preferred_element_type=jnp.float32)
        dv_part = lax.dot_general(probs_low, g, tn, preferred_element_type=jnp.float32)
        dk_acc = dk_part if dk_acc is None else dk_acc + dk_part
        dv_acc = dv_part if dv_acc is None else dv_acc + dv_part
    acc_start = pl.multiple_of(start - acc_base, rows)
    dk_ref[pl.ds(acc_start, span), :] += dk_acc
    dv_ref[pl.ds(acc_start, span), :] += dv_acc
    if early:

        @pl.when(step == pl.num_programs(0) - 1)
        def _():
            halo_ref[:, :HD] = dk_ref[:WIN, :].astype(jnp.bfloat16)
            halo_ref[:, HD:] = dv_ref[:WIN, :].astype(jnp.bfloat16)


def attend(sources, first_part, tail, first_query, blocks, carried_od):
    heads = len(sources)
    query_count = first_part.shape[0]
    acc_base = 0 if tail is not None else WIN
    acc_rows = 2 * WIN if tail is not None else query_count
    rows = BLK
    span = WIN + rows
    block_offset, block_count = blocks
    early = tail is not None
    first = jnp.reshape(first_query, (1,)).astype(jnp.int32)
    whole = pl.BlockSpec((acc_rows, HD), lambda b, f: (0, 0))
    in_specs = []
    operands = [first]
    for source, q_col, g_col in sources:
        in_specs += [
            pl.BlockSpec((rows, HD), lambda b, f, c=q_col: (b + block_offset, c)),
            pl.BlockSpec((rows, HD), lambda b, f, c=g_col: (b + block_offset, c)),
        ]
        operands += [source, source]
    if early:
        piece = (WIN, HD)
        in_specs += [
            pl.BlockSpec(piece, lambda b, f: (0, 0)),
            pl.BlockSpec(piece, lambda b, f: (0, 1)),
            pl.BlockSpec(piece, lambda b, f: (0, 0)),
            pl.BlockSpec(piece, lambda b, f: (0, 1)),
        ]
        operands += [tail, tail, first_part, first_part]
    else:
        in_specs += [
            pl.BlockSpec((query_count, HD), lambda b, f: (0, 0)),
            pl.BlockSpec((query_count, HD), lambda b, f: (0, 1)),
        ]
        operands += [first_part, first_part]
    aliases = {}
    carry_od = tuple(od is not None for od in carried_od)
    for i, od in enumerate(carried_od):
        if od is not None:
            aliases[len(operands)] = i
            in_specs.append(pl.BlockSpec(memory_space=pl.ANY))
            operands.append(od)
    scratch = [pltpu.VMEM((rows, span), jnp.float32)]
    if early:
        scratch += [pltpu.VMEM((2 * WIN, HD), jnp.bfloat16)] * 2
    grid_spec = pltpu.PrefetchScalarGridSpec(
        num_scalar_prefetch=1,
        grid=(block_count,),
        in_specs=in_specs,
        out_specs=[pl.BlockSpec((rows, 2 * HD), lambda b, f: (b + block_offset, 0))] * heads
        + [whole, whole]
        + ([pl.BlockSpec((WIN, 2 * HD), lambda b, f: (0, 0))] if early else []),
        scratch_shapes=scratch,
    )
    kernel = functools.partial(
        attend_kernel,
        heads=heads,
        block_offset=block_offset,
        early=early,
        carry_od=carry_od,
        acc_base=acc_base,
    )
    return pl.pallas_call(
        kernel,
        grid_spec=grid_spec,
        out_shape=[jax.ShapeDtypeStruct((query_count, 2 * HD), jnp.bfloat16)] * heads
        + [
            jax.ShapeDtypeStruct((acc_rows, HD), jnp.float32),
            jax.ShapeDtypeStruct((acc_rows, HD), jnp.float32),
        ]
        + ([jax.ShapeDtypeStruct((WIN, 2 * HD), jnp.bfloat16)] if early else []),
        input_output_aliases=aliases,
        compiler_params=pltpu.CompilerParams(
            dimension_semantics=("arbitrary",), vmem_limit_bytes=56 * 1024 * 1024
        ),
    )(*operands)


def exchange_in(pieces):
    stacked = jnp.transpose(jnp.concatenate(pieces, axis=-1), (1, 0, 2))
    moved = lax.all_to_all(stacked, "head", split_axis=0, concat_axis=0, tiled=True)
    return moved.reshape(moved.shape[0] * moved.shape[1], moved.shape[2])


def exchange_out(group_block):
    shared = lax.axis_size("head")
    split = group_block.reshape(shared, group_block.shape[0] // shared, group_block.shape[1])
    moved = lax.all_to_all(split, "head", split_axis=0, concat_axis=0, tiled=True)
    return jnp.transpose(moved, (1, 0, 2))


def body(queries, keys, values, grad_out):
    token_count = queries.shape[0]
    shared = KVH
    pair = (QH // KVH) * HD
    query_rows = queries.reshape(token_count, shared, pair)
    grad_rows = grad_out.reshape(token_count, shared, pair)
    key_rows = keys.reshape(token_count, shared, HD)
    value_rows = values.reshape(token_count, shared, HD)
    first_part = exchange_in(
        [key_rows, value_rows, query_rows[:, :, :HD], grad_rows[:, :, :HD]]
    )
    second_part = exchange_in([query_rows[:, :, HD:], grad_rows[:, :, HD:]])
    group_rows = first_part.shape[0]
    block_total = group_rows // BLK
    lead = WIN // BLK
    first_query = lax.axis_index("ctx") * group_rows
    tail = shifted(first_part[group_rows - WIN :, : 2 * HD], "ctx", 1)
    late = (lead, block_total - lead)
    early = (0, lead)
    head0 = (first_part, 2, 3)
    head1 = (second_part, 0, 1)
    first_out, key_late, value_late = attend([head0], first_part, None, first_query, late, (None,))
    first_out, second_out, key_early, value_early, halo_part = attend(
        [head0, head1], first_part, tail, first_query, early, (first_out, None)
    )
    back = shifted(halo_part, "ctx", -1).astype(jnp.float32)
    second_out, key_last, value_last = attend(
        [head1], first_part, None, first_query, late, (second_out,)
    )
    first_back = exchange_out(first_out)
    second_back = exchange_out(second_out)
    lead_pad = ((0, group_rows - WIN), (0, 0))
    tail_pad = ((group_rows - WIN, 0), (0, 0))
    key_grad = (
        key_late + key_last + jnp.pad(key_early[WIN:], lead_pad) + jnp.pad(back[:, :HD], tail_pad)
    ).astype(jnp.bfloat16)
    value_grad = (
        value_late
        + value_last
        + jnp.pad(value_early[WIN:], lead_pad)
        + jnp.pad(back[:, HD:], tail_pad)
    ).astype(jnp.bfloat16)
    grads_back = exchange_out(jnp.concatenate([key_grad, value_grad], axis=1))
    attended = jnp.concatenate([first_back[:, :, :HD], second_back[:, :, :HD]], axis=2)
    grad_queries = jnp.concatenate([first_back[:, :, HD:], second_back[:, :, HD:]], axis=2)
    return (
        attended.reshape(token_count, QH * HD),
        grad_queries.reshape(token_count, QH * HD),
        grads_back[:, :, :HD].reshape(token_count, KVH * HD),
        grads_back[:, :, HD:].reshape(token_count, KVH * HD),
    )


def solution(mesh):
    placed = (
        P(("ctx", "head"), None),
        P(("ctx", "head"), None),
        P(("ctx", "head"), None),
        P(("ctx", "head"), None),
    )
    return jax.shard_map(
        body,
        mesh=mesh,
        in_specs=placed,
        out_specs=(
            P(("ctx", "head"), None),
            P(("ctx", "head"), None),
            P(("ctx", "head"), None),
            P(("ctx", "head"), None),
        ),
        check_vma=False,
    )
```

```python
import functools

import jax
import jax.numpy as jnp
from jax import lax
from jax.experimental import pallas as pl
from jax.experimental.pallas import tpu as pltpu
from jax.sharding import PartitionSpec as P

HD = 128
QH = 32
KVH = 16
WIN = 1024
QPRE = 168
BLK = 256


def shifted(block, axis, distance):
    devices = range(lax.axis_size(axis))
    route = [(i - distance, i) for i in devices if i - distance in devices]
    return lax.ppermute(block, axis, route)


def attend_kernel(first_ref, *refs, heads, block_offset, early, carry_od, acc_base):
    pos = 0
    q_refs, g_refs = [], []
    for _ in range(heads):
        q_refs.append(refs[pos])
        g_refs.append(refs[pos + 1])
        pos += 2
    if early:
        kt_ref, vt_ref, kg_ref, vg_ref = refs[pos : pos + 4]
        pos += 4
    else:
        k_ref, v_ref = refs[pos : pos + 2]
        pos += 2
    pos += sum(carry_od)
    od_refs = refs[pos : pos + heads]
    pos += heads
    dk_ref, dv_ref = refs[pos : pos + 2]
    pos += 2
    if early:
        halo_ref = refs[pos]
        pos += 1
    bias_ref = refs[pos]
    pos += 1
    if early:
        kx_ref, vx_ref, dkx_ref, dvx_ref = refs[pos : pos + 4]
        dk_out_ref, dv_out_ref = dk_ref, dv_ref
        dk_ref, dv_ref = dkx_ref, dvx_ref
    step = pl.program_id(0)
    block = step + block_offset
    rows = q_refs[0].shape[0]
    span = WIN + rows
    scale = QPRE ** (-0.5)

    @pl.when(step == 0)
    def _():
        dk_ref[...] = jnp.zeros_like(dk_ref)
        dv_ref[...] = jnp.zeros_like(dv_ref)
        row_id = lax.broadcasted_iota(jnp.int32, (rows, span), 0)
        col_id = lax.broadcasted_iota(jnp.int32, (rows, span), 1)
        distance = row_id + WIN - col_id
        band = (distance >= 0) & (distance < WIN)
        bias_ref[...] = jnp.where(band, 0.0, -jnp.inf).astype(jnp.float32)
        if early:
            kx_ref[:WIN, :] = kt_ref[...]
            kx_ref[WIN:, :] = kg_ref[...]
            vx_ref[:WIN, :] = vt_ref[...]
            vx_ref[WIN:, :] = vg_ref[...]

    start = pl.multiple_of(block * rows, rows)
    if early:
        k_win = kx_ref[pl.ds(start, span), :]
        v_win = vx_ref[pl.ds(start, span), :]
        col_id = lax.broadcasted_iota(jnp.int32, (rows, span), 1)
        key_pos = first_ref[0] - WIN + start + col_id
        bias = jnp.where(key_pos >= 0, bias_ref[...], -jnp.inf)
    else:
        key_start = pl.multiple_of(start - WIN, rows)
        k_win = k_ref[pl.ds(key_start, span), :]
        v_win = v_ref[pl.ds(key_start, span), :]
        bias = bias_ref[...]
    nt = (((1,), (1,)), ((), ()))
    tn = (((0,), (0,)), ((), ()))
    dk_acc = None
    dv_acc = None
    for q_ref, g_ref, od_ref in zip(q_refs, g_refs, od_refs):
        q = q_ref[...]
        g = g_ref[...]
        scores = lax.dot_general(q, k_win, nt, preferred_element_type=jnp.float32) * scale
        scores = scores + bias
        largest = jnp.max(scores, axis=-1, keepdims=True)
        unnormed = jnp.exp(scores - largest)
        probs = unnormed * (1.0 / jnp.sum(unnormed, axis=-1, keepdims=True))
        probs_low = probs.astype(jnp.bfloat16)
        out = jnp.dot(probs_low, v_win, preferred_element_type=jnp.float32).astype(jnp.bfloat16)
        od_ref[:, :HD] = out
        grad_probs = lax.dot_general(g, v_win, nt, preferred_element_type=jnp.float32)
        inner = jnp.sum(g.astype(jnp.float32) * out.astype(jnp.float32), axis=-1, keepdims=True)
        grad_scores = (probs * (grad_probs - inner) * scale).astype(jnp.bfloat16)
        od_ref[:, HD:] = jnp.dot(grad_scores, k_win, preferred_element_type=jnp.float32).astype(
            jnp.bfloat16
        )
        dk_part = lax.dot_general(grad_scores, q, tn, preferred_element_type=jnp.float32)
        dv_part = lax.dot_general(probs_low, g, tn, preferred_element_type=jnp.float32)
        dk_acc = dk_part if dk_acc is None else dk_acc + dk_part
        dv_acc = dv_part if dv_acc is None else dv_acc + dv_part
    acc_start = pl.multiple_of(start - acc_base, rows)
    dk_ref[pl.ds(acc_start, span), :] += dk_acc
    dv_ref[pl.ds(acc_start, span), :] += dv_acc
    if early:

        @pl.when(step == pl.num_programs(0) - 1)
        def _():
            halo_ref[:, :HD] = dk_ref[:WIN, :].astype(jnp.bfloat16)
            halo_ref[:, HD:] = dv_ref[:WIN, :].astype(jnp.bfloat16)
            dk_out_ref[...] = dk_ref[WIN:, :]
            dv_out_ref[...] = dv_ref[WIN:, :]


def attend(sources, first_part, tail, first_query, blocks, carried_od):
    heads = len(sources)
    query_count = first_part.shape[0]
    acc_base = 0 if tail is not None else WIN
    acc_rows = WIN if tail is not None else query_count
    rows = BLK
    span = WIN + rows
    block_offset, block_count = blocks
    early = tail is not None
    first = jnp.reshape(first_query, (1,)).astype(jnp.int32)
    whole = pl.BlockSpec((acc_rows, HD), lambda b, f: (0, 0))
    in_specs = []
    operands = [first]
    for source, q_col, g_col in sources:
        in_specs += [
            pl.BlockSpec((rows, HD), lambda b, f, c=q_col: (b + block_offset, c)),
            pl.BlockSpec((rows, HD), lambda b, f, c=g_col: (b + block_offset, c)),
        ]
        operands += [source, source]
    if early:
        piece = (WIN, HD)
        in_specs += [
            pl.BlockSpec(piece, lambda b, f: (0, 0)),
            pl.BlockSpec(piece, lambda b, f: (0, 1)),
            pl.BlockSpec(piece, lambda b, f: (0, 0)),
            pl.BlockSpec(piece, lambda b, f: (0, 1)),
        ]
        operands += [tail, tail, first_part, first_part]
    else:
        in_specs += [
            pl.BlockSpec((query_count, HD), lambda b, f: (0, 0)),
            pl.BlockSpec((query_count, HD), lambda b, f: (0, 1)),
        ]
        operands += [first_part, first_part]
    aliases = {}
    carry_od = tuple(od is not None for od in carried_od)
    for i, od in enumerate(carried_od):
        if od is not None:
            aliases[len(operands)] = i
            in_specs.append(pl.BlockSpec(memory_space=pl.ANY))
            operands.append(od)
    scratch = [pltpu.VMEM((rows, span), jnp.float32)]
    if early:
        scratch += [pltpu.VMEM((2 * WIN, HD), jnp.bfloat16)] * 2
        scratch += [pltpu.VMEM((2 * WIN, HD), jnp.float32)] * 2
    grid_spec = pltpu.PrefetchScalarGridSpec(
        num_scalar_prefetch=1,
        grid=(block_count,),
        in_specs=in_specs,
        out_specs=[pl.BlockSpec((rows, 2 * HD), lambda b, f: (b + block_offset, 0))] * heads
        + [whole, whole]
        + ([pl.BlockSpec((WIN, 2 * HD), lambda b, f: (0, 0))] if early else []),
        scratch_shapes=scratch,
    )
    kernel = functools.partial(
        attend_kernel,
        heads=heads,
        block_offset=block_offset,
        early=early,
        carry_od=carry_od,
        acc_base=acc_base,
    )
    return pl.pallas_call(
        kernel,
        grid_spec=grid_spec,
        out_shape=[jax.ShapeDtypeStruct((query_count, 2 * HD), jnp.bfloat16)] * heads
        + [
            jax.ShapeDtypeStruct((acc_rows, HD), jnp.float32),
            jax.ShapeDtypeStruct((acc_rows, HD), jnp.float32),
        ]
        + ([jax.ShapeDtypeStruct((WIN, 2 * HD), jnp.bfloat16)] if early else []),
        input_output_aliases=aliases,
        compiler_params=pltpu.CompilerParams(
            dimension_semantics=("arbitrary",), vmem_limit_bytes=56 * 1024 * 1024
        ),
    )(*operands)


def exchange_in(pieces):
    stacked = jnp.transpose(jnp.concatenate(pieces, axis=-1), (1, 0, 2))
    moved = lax.all_to_all(stacked, "head", split_axis=0, concat_axis=0, tiled=True)
    return moved.reshape(moved.shape[0] * moved.shape[1], moved.shape[2])


def exchange_out(group_block):
    shared = lax.axis_size("head")
    split = group_block.reshape(shared, group_block.shape[0] // shared, group_block.shape[1])
    moved = lax.all_to_all(split, "head", split_axis=0, concat_axis=0, tiled=True)
    return jnp.transpose(moved, (1, 0, 2))


def body(queries, keys, values, grad_out):
    token_count = queries.shape[0]
    shared = KVH
    pair = (QH // KVH) * HD
    query_rows = queries.reshape(token_count, shared, pair)
    grad_rows = grad_out.reshape(token_count, shared, pair)
    key_rows = keys.reshape(token_count, shared, HD)
    value_rows = values.reshape(token_count, shared, HD)
    first_part = exchange_in(
        [key_rows, value_rows, query_rows[:, :, :HD], grad_rows[:, :, :HD]]
    )
    second_part = exchange_in([query_rows[:, :, HD:], grad_rows[:, :, HD:]])
    group_rows = first_part.shape[0]
    block_total = group_rows // BLK
    lead = WIN // BLK
    first_query = lax.axis_index("ctx") * group_rows
    tail = shifted(first_part[group_rows - WIN :, : 2 * HD], "ctx", 1)
    late = (lead, block_total - lead)
    early = (0, lead)
    head0 = (first_part, 2, 3)
    head1 = (second_part, 0, 1)
    first_out, key_late, value_late = attend([head0], first_part, None, first_query, late, (None,))
    first_out, second_out, key_early, value_early, halo_part = attend(
        [head0, head1], first_part, tail, first_query, early, (first_out, None)
    )
    back = shifted(halo_part, "ctx", -1).astype(jnp.float32)
    second_out, key_last, value_last = attend(
        [head1], first_part, None, first_query, late, (second_out,)
    )
    first_back = exchange_out(first_out)
    second_back = exchange_out(second_out)
    lead_pad = ((0, group_rows - WIN), (0, 0))
    tail_pad = ((group_rows - WIN, 0), (0, 0))
    key_grad = (
        key_late + key_last + jnp.pad(key_early, lead_pad) + jnp.pad(back[:, :HD], tail_pad)
    ).astype(jnp.bfloat16)
    value_grad = (
        value_late
        + value_last
        + jnp.pad(value_early, lead_pad)
        + jnp.pad(back[:, HD:], tail_pad)
    ).astype(jnp.bfloat16)
    grads_back = exchange_out(jnp.concatenate([key_grad, value_grad], axis=1))
    attended = jnp.concatenate([first_back[:, :, :HD], second_back[:, :, :HD]], axis=2)
    grad_queries = jnp.concatenate([first_back[:, :, HD:], second_back[:, :, HD:]], axis=2)
    return (
        attended.reshape(token_count, QH * HD),
        grad_queries.reshape(token_count, QH * HD),
        grads_back[:, :, :HD].reshape(token_count, KVH * HD),
        grads_back[:, :, HD:].reshape(token_count, KVH * HD),
    )


def solution(mesh):
    placed = (
        P(("ctx", "head"), None),
        P(("ctx", "head"), None),
        P(("ctx", "head"), None),
        P(("ctx", "head"), None),
    )
    return jax.shard_map(
        body,
        mesh=mesh,
        in_specs=placed,
        out_specs=(
            P(("ctx", "head"), None),
            P(("ctx", "head"), None),
            P(("ctx", "head"), None),
            P(("ctx", "head"), None),
        ),
        check_vma=False,
    )
```

```python
import functools

import jax
import jax.numpy as jnp
from jax import lax
from jax.experimental import pallas as pl
from jax.experimental.pallas import tpu as pltpu
from jax.sharding import PartitionSpec as P

HD = 128
QH = 32
KVH = 16
WIN = 1024
QPRE = 168
BLK = 256


def shifted(block, axis, distance):
    devices = range(lax.axis_size(axis))
    route = [(i - distance, i) for i in devices if i - distance in devices]
    return lax.ppermute(block, axis, route)


def attend_kernel(first_ref, *refs, heads, block_offset, early, carry_od, acc_base):
    pos = 0
    q_refs, g_refs = [], []
    for _ in range(heads):
        q_refs.append(refs[pos])
        g_refs.append(refs[pos + 1])
        pos += 2
    if early:
        kt_ref, vt_ref, kg_ref, vg_ref = refs[pos : pos + 4]
        pos += 4
    else:
        k_ref, v_ref = refs[pos : pos + 2]
        pos += 2
    pos += sum(carry_od)
    od_refs = refs[pos : pos + heads]
    pos += heads
    dk_ref, dv_ref = refs[pos : pos + 2]
    pos += 2
    if early:
        halo_ref = refs[pos]
        pos += 1
    bias_ref = refs[pos]
    pos += 1
    if early:
        kx_ref, vx_ref, dkx_ref, dvx_ref = refs[pos : pos + 4]
        dk_out_ref, dv_out_ref = dk_ref, dv_ref
        dk_ref, dv_ref = dkx_ref, dvx_ref
    step = pl.program_id(0)
    block = step + block_offset
    rows = q_refs[0].shape[0]
    span = WIN + rows
    scale = QPRE ** (-0.5)

    @pl.when(step == 0)
    def _():
        dk_ref[...] = jnp.zeros_like(dk_ref)
        dv_ref[...] = jnp.zeros_like(dv_ref)
        row_id = lax.broadcasted_iota(jnp.int32, (rows, span), 0)
        col_id = lax.broadcasted_iota(jnp.int32, (rows, span), 1)
        distance = row_id + WIN - col_id
        band = (distance >= 0) & (distance < WIN)
        bias_ref[...] = jnp.where(band, 0.0, -jnp.inf).astype(jnp.float32)
        if early:
            kx_ref[:WIN, :] = kt_ref[...]
            kx_ref[WIN:, :] = kg_ref[...]
            vx_ref[:WIN, :] = vt_ref[...]
            vx_ref[WIN:, :] = vg_ref[...]

    start = pl.multiple_of(block * rows, rows)
    if early:
        k_win = kx_ref[pl.ds(start, span), :]
        v_win = vx_ref[pl.ds(start, span), :]
        col_id = lax.broadcasted_iota(jnp.int32, (rows, span), 1)
        key_pos = first_ref[0] - WIN + start + col_id
        bias = jnp.where(key_pos >= 0, bias_ref[...], -jnp.inf)
    else:
        key_start = pl.multiple_of(start - WIN, rows)
        k_win = k_ref[pl.ds(key_start, span), :]
        v_win = v_ref[pl.ds(key_start, span), :]
        bias = bias_ref[...]
    nt = (((1,), (1,)), ((), ()))
    tn = (((0,), (0,)), ((), ()))
    dk_acc = None
    dv_acc = None
    for q_ref, g_ref, od_ref in zip(q_refs, g_refs, od_refs):
        q = q_ref[...]
        g = g_ref[...]
        scores = lax.dot_general(q, k_win, nt, preferred_element_type=jnp.float32) * scale
        scores = scores + bias
        largest = jnp.max(scores, axis=-1, keepdims=True)
        unnormed = jnp.exp(scores - largest)
        probs = unnormed * (1.0 / jnp.sum(unnormed, axis=-1, keepdims=True))
        probs_low = probs.astype(jnp.bfloat16)
        out = jnp.dot(probs_low, v_win, preferred_element_type=jnp.float32).astype(jnp.bfloat16)
        od_ref[:, :HD] = out
        grad_probs = lax.dot_general(g, v_win, nt, preferred_element_type=jnp.float32)
        inner = jnp.sum(g.astype(jnp.float32) * out.astype(jnp.float32), axis=-1, keepdims=True)
        grad_scores = (probs * (grad_probs - inner) * scale).astype(jnp.bfloat16)
        od_ref[:, HD:] = jnp.dot(grad_scores, k_win, preferred_element_type=jnp.float32).astype(
            jnp.bfloat16
        )
        dk_part = lax.dot_general(grad_scores, q, tn, preferred_element_type=jnp.float32)
        dv_part = lax.dot_general(probs_low, g, tn, preferred_element_type=jnp.float32)
        dk_acc = dk_part if dk_acc is None else dk_acc + dk_part
        dv_acc = dv_part if dv_acc is None else dv_acc + dv_part
    acc_start = pl.multiple_of(start - acc_base, rows)
    dk_ref[pl.ds(acc_start, span), :] += dk_acc
    dv_ref[pl.ds(acc_start, span), :] += dv_acc
    if early:

        @pl.when(step == pl.num_programs(0) - 1)
        def _():
            halo_ref[:, :HD] = dk_ref[:WIN, :]
            halo_ref[:, HD:] = dv_ref[:WIN, :]
            dk_out_ref[...] = dk_ref[WIN:, :]
            dv_out_ref[...] = dv_ref[WIN:, :]


def attend(sources, first_part, tail, first_query, blocks, carried_od):
    heads = len(sources)
    query_count = first_part.shape[0]
    acc_base = 0 if tail is not None else WIN
    acc_rows = WIN if tail is not None else query_count
    rows = BLK
    span = WIN + rows
    block_offset, block_count = blocks
    early = tail is not None
    first = jnp.reshape(first_query, (1,)).astype(jnp.int32)
    whole = pl.BlockSpec((acc_rows, HD), lambda b, f: (0, 0))
    in_specs = []
    operands = [first]
    for source, q_col, g_col in sources:
        in_specs += [
            pl.BlockSpec((rows, HD), lambda b, f, c=q_col: (b + block_offset, c)),
            pl.BlockSpec((rows, HD), lambda b, f, c=g_col: (b + block_offset, c)),
        ]
        operands += [source, source]
    if early:
        piece = (WIN, HD)
        in_specs += [
            pl.BlockSpec(piece, lambda b, f: (0, 0)),
            pl.BlockSpec(piece, lambda b, f: (0, 1)),
            pl.BlockSpec(piece, lambda b, f: (0, 0)),
            pl.BlockSpec(piece, lambda b, f: (0, 1)),
        ]
        operands += [tail, tail, first_part, first_part]
    else:
        in_specs += [
            pl.BlockSpec((query_count, HD), lambda b, f: (0, 0)),
            pl.BlockSpec((query_count, HD), lambda b, f: (0, 1)),
        ]
        operands += [first_part, first_part]
    aliases = {}
    carry_od = tuple(od is not None for od in carried_od)
    for i, od in enumerate(carried_od):
        if od is not None:
            aliases[len(operands)] = i
            in_specs.append(pl.BlockSpec(memory_space=pl.ANY))
            operands.append(od)
    scratch = [pltpu.VMEM((rows, span), jnp.float32)]
    if early:
        scratch += [pltpu.VMEM((2 * WIN, HD), jnp.bfloat16)] * 2
        scratch += [pltpu.VMEM((2 * WIN, HD), jnp.float32)] * 2
    grid_spec = pltpu.PrefetchScalarGridSpec(
        num_scalar_prefetch=1,
        grid=(block_count,),
        in_specs=in_specs,
        out_specs=[pl.BlockSpec((rows, 2 * HD), lambda b, f: (b + block_offset, 0))] * heads
        + [whole, whole]
        + ([pl.BlockSpec((WIN, 2 * HD), lambda b, f: (0, 0))] if early else []),
        scratch_shapes=scratch,
    )
    kernel = functools.partial(
        attend_kernel,
        heads=heads,
        block_offset=block_offset,
        early=early,
        carry_od=carry_od,
        acc_base=acc_base,
    )
    return pl.pallas_call(
        kernel,
        grid_spec=grid_spec,
        out_shape=[jax.ShapeDtypeStruct((query_count, 2 * HD), jnp.bfloat16)] * heads
        + [
            jax.ShapeDtypeStruct((acc_rows, HD), jnp.float32),
            jax.ShapeDtypeStruct((acc_rows, HD), jnp.float32),
        ]
        + ([jax.ShapeDtypeStruct((WIN, 2 * HD), jnp.float32)] if early else []),
        input_output_aliases=aliases,
        compiler_params=pltpu.CompilerParams(
            dimension_semantics=("arbitrary",), vmem_limit_bytes=56 * 1024 * 1024
        ),
    )(*operands)


def exchange_in(pieces):
    stacked = jnp.transpose(jnp.concatenate(pieces, axis=-1), (1, 0, 2))
    moved = lax.all_to_all(stacked, "head", split_axis=0, concat_axis=0, tiled=True)
    return moved.reshape(moved.shape[0] * moved.shape[1], moved.shape[2])


def exchange_out(group_block):
    shared = lax.axis_size("head")
    split = group_block.reshape(shared, group_block.shape[0] // shared, group_block.shape[1])
    moved = lax.all_to_all(split, "head", split_axis=0, concat_axis=0, tiled=True)
    return jnp.transpose(moved, (1, 0, 2))


def body(queries, keys, values, grad_out):
    token_count = queries.shape[0]
    shared = KVH
    pair = (QH // KVH) * HD
    query_rows = queries.reshape(token_count, shared, pair)
    grad_rows = grad_out.reshape(token_count, shared, pair)
    key_rows = keys.reshape(token_count, shared, HD)
    value_rows = values.reshape(token_count, shared, HD)
    first_part = exchange_in(
        [key_rows, value_rows, query_rows[:, :, :HD], grad_rows[:, :, :HD]]
    )
    second_part = exchange_in([query_rows[:, :, HD:], grad_rows[:, :, HD:]])
    group_rows = first_part.shape[0]
    block_total = group_rows // BLK
    lead = WIN // BLK
    first_query = lax.axis_index("ctx") * group_rows
    tail = shifted(first_part[group_rows - WIN :, : 2 * HD], "ctx", 1)
    late = (lead, block_total - lead)
    early = (0, lead)
    head0 = (first_part, 2, 3)
    head1 = (second_part, 0, 1)
    first_out, key_late, value_late = attend([head0], first_part, None, first_query, late, (None,))
    first_out, key_early0, value_early0, halo0 = attend(
        [head0], first_part, tail, first_query, early, (first_out,)
    )
    second_out, key_early1, value_early1, halo1 = attend(
        [head1], first_part, tail, first_query, early, (None,)
    )
    key_early = key_early0 + key_early1
    value_early = value_early0 + value_early1
    halo_part = (halo0 + halo1).astype(jnp.bfloat16)
    back = shifted(halo_part, "ctx", -1).astype(jnp.float32)
    second_out, key_last, value_last = attend(
        [head1], first_part, None, first_query, late, (second_out,)
    )
    first_back = exchange_out(first_out)
    second_back = exchange_out(second_out)
    lead_pad = ((0, group_rows - WIN), (0, 0))
    tail_pad = ((group_rows - WIN, 0), (0, 0))
    key_grad = (
        key_late + key_last + jnp.pad(key_early, lead_pad) + jnp.pad(back[:, :HD], tail_pad)
    ).astype(jnp.bfloat16)
    value_grad = (
        value_late
        + value_last
        + jnp.pad(value_early, lead_pad)
        + jnp.pad(back[:, HD:], tail_pad)
    ).astype(jnp.bfloat16)
    grads_back = exchange_out(jnp.concatenate([key_grad, value_grad], axis=1))
    attended = jnp.concatenate([first_back[:, :, :HD], second_back[:, :, :HD]], axis=2)
    grad_queries = jnp.concatenate([first_back[:, :, HD:], second_back[:, :, HD:]], axis=2)
    return (
        attended.reshape(token_count, QH * HD),
        grad_queries.reshape(token_count, QH * HD),
        grads_back[:, :, :HD].reshape(token_count, KVH * HD),
        grads_back[:, :, HD:].reshape(token_count, KVH * HD),
    )


def solution(mesh):
    placed = (
        P(("ctx", "head"), None),
        P(("ctx", "head"), None),
        P(("ctx", "head"), None),
        P(("ctx", "head"), None),
    )
    return jax.shard_map(
        body,
        mesh=mesh,
        in_specs=placed,
        out_specs=(
            P(("ctx", "head"), None),
            P(("ctx", "head"), None),
            P(("ctx", "head"), None),
            P(("ctx", "head"), None),
        ),
        check_vma=False,
    )
```

```python
import functools

import jax
import jax.numpy as jnp
from jax import lax
from jax.experimental import pallas as pl
from jax.experimental.pallas import tpu as pltpu
from jax.sharding import PartitionSpec as P

HD = 128
QH = 32
KVH = 16
WIN = 1024
QPRE = 168
BLK = 256


def shifted(block, axis, distance):
    devices = range(lax.axis_size(axis))
    route = [(i - distance, i) for i in devices if i - distance in devices]
    return lax.ppermute(block, axis, route)


def attend_kernel(first_ref, *refs, heads, block_offset, early, carry_od, acc_base):
    pos = 0
    q_refs, g_refs = [], []
    for _ in range(heads):
        q_refs.append(refs[pos])
        g_refs.append(refs[pos + 1])
        pos += 2
    if early:
        kt_ref, vt_ref, kg_ref, vg_ref = refs[pos : pos + 4]
        pos += 4
    else:
        k_ref, v_ref = refs[pos : pos + 2]
        pos += 2
    pos += sum(carry_od)
    od_refs = refs[pos : pos + heads]
    pos += heads
    dk_ref, dv_ref = refs[pos : pos + 2]
    pos += 2
    if early:
        halo_ref = refs[pos]
        pos += 1
    bias_ref = refs[pos]
    pos += 1
    if early:
        kx_ref, vx_ref, dkx_ref, dvx_ref = refs[pos : pos + 4]
        dk_out_ref, dv_out_ref = dk_ref, dv_ref
        dk_ref, dv_ref = dkx_ref, dvx_ref
    step = pl.program_id(0)
    block = step + block_offset
    rows = q_refs[0].shape[0]
    span = WIN + rows
    scale = QPRE ** (-0.5)

    @pl.when(step == 0)
    def _():
        dk_ref[...] = jnp.zeros_like(dk_ref)
        dv_ref[...] = jnp.zeros_like(dv_ref)
        row_id = lax.broadcasted_iota(jnp.int32, (rows, span), 0)
        col_id = lax.broadcasted_iota(jnp.int32, (rows, span), 1)
        distance = row_id + WIN - col_id
        band = (distance >= 0) & (distance < WIN)
        bias_ref[...] = jnp.where(band, 0.0, -jnp.inf).astype(jnp.float32)
        if early:
            kx_ref[:WIN, :] = kt_ref[...]
            kx_ref[WIN:, :] = kg_ref[...]
            vx_ref[:WIN, :] = vt_ref[...]
            vx_ref[WIN:, :] = vg_ref[...]

    start = pl.multiple_of(block * rows, rows)
    if early:
        k_win = kx_ref[pl.ds(start, span), :]
        v_win = vx_ref[pl.ds(start, span), :]
        col_id = lax.broadcasted_iota(jnp.int32, (rows, span), 1)
        key_pos = first_ref[0] - WIN + start + col_id
        bias = jnp.where(key_pos >= 0, bias_ref[...], -jnp.inf)
    else:
        key_start = pl.multiple_of(start - WIN, rows)
        k_win = k_ref[pl.ds(key_start, span), :]
        v_win = v_ref[pl.ds(key_start, span), :]
        bias = bias_ref[...]
    nt = (((1,), (1,)), ((), ()))
    tn = (((0,), (0,)), ((), ()))
    q = jnp.concatenate([r[...] for r in q_refs], axis=0)
    g = jnp.concatenate([r[...] for r in g_refs], axis=0)
    scores = lax.dot_general(q, k_win, nt, preferred_element_type=jnp.float32) * scale
    scores = (scores.reshape(heads, rows, span) + bias[None]).reshape(heads * rows, span)
    largest = jnp.max(scores, axis=-1, keepdims=True)
    unnormed = jnp.exp(scores - largest)
    probs = unnormed * (1.0 / jnp.sum(unnormed, axis=-1, keepdims=True))
    probs_low = probs.astype(jnp.bfloat16)
    out = jnp.dot(probs_low, v_win, preferred_element_type=jnp.float32).astype(jnp.bfloat16)
    grad_probs = lax.dot_general(g, v_win, nt, preferred_element_type=jnp.float32)
    inner = jnp.sum(g.astype(jnp.float32) * out.astype(jnp.float32), axis=-1, keepdims=True)
    grad_scores = (probs * (grad_probs - inner) * scale).astype(jnp.bfloat16)
    grad_query = jnp.dot(grad_scores, k_win, preferred_element_type=jnp.float32).astype(
        jnp.bfloat16
    )
    for h, od_ref in enumerate(od_refs):
        od_ref[:, :HD] = out[h * rows : (h + 1) * rows]
        od_ref[:, HD:] = grad_query[h * rows : (h + 1) * rows]
    dk_acc = lax.dot_general(grad_scores, q, tn, preferred_element_type=jnp.float32)
    dv_acc = lax.dot_general(probs_low, g, tn, preferred_element_type=jnp.float32)
    acc_start = pl.multiple_of(start - acc_base, rows)
    dk_ref[pl.ds(acc_start, span), :] += dk_acc
    dv_ref[pl.ds(acc_start, span), :] += dv_acc
    if early:

        @pl.when(step == pl.num_programs(0) - 1)
        def _():
            halo_ref[:, :HD] = dk_ref[:WIN, :].astype(jnp.bfloat16)
            halo_ref[:, HD:] = dv_ref[:WIN, :].astype(jnp.bfloat16)
            dk_out_ref[...] = dk_ref[WIN:, :]
            dv_out_ref[...] = dv_ref[WIN:, :]


def attend(sources, first_part, tail, first_query, blocks, carried_od):
    heads = len(sources)
    query_count = first_part.shape[0]
    acc_base = 0 if tail is not None else WIN
    acc_rows = WIN if tail is not None else query_count
    rows = BLK
    span = WIN + rows
    block_offset, block_count = blocks
    early = tail is not None
    first = jnp.reshape(first_query, (1,)).astype(jnp.int32)
    whole = pl.BlockSpec((acc_rows, HD), lambda b, f: (0, 0))
    in_specs = []
    operands = [first]
    for source, q_col, g_col in sources:
        in_specs += [
            pl.BlockSpec((rows, HD), lambda b, f, c=q_col: (b + block_offset, c)),
            pl.BlockSpec((rows, HD), lambda b, f, c=g_col: (b + block_offset, c)),
        ]
        operands += [source, source]
    if early:
        piece = (WIN, HD)
        in_specs += [
            pl.BlockSpec(piece, lambda b, f: (0, 0)),
            pl.BlockSpec(piece, lambda b, f: (0, 1)),
            pl.BlockSpec(piece, lambda b, f: (0, 0)),
            pl.BlockSpec(piece, lambda b, f: (0, 1)),
        ]
        operands += [tail, tail, first_part, first_part]
    else:
        in_specs += [
            pl.BlockSpec((query_count, HD), lambda b, f: (0, 0)),
            pl.BlockSpec((query_count, HD), lambda b, f: (0, 1)),
        ]
        operands += [first_part, first_part]
    aliases = {}
    carry_od = tuple(od is not None for od in carried_od)
    for i, od in enumerate(carried_od):
        if od is not None:
            aliases[len(operands)] = i
            in_specs.append(pl.BlockSpec(memory_space=pl.ANY))
            operands.append(od)
    scratch = [pltpu.VMEM((rows, span), jnp.float32)]
    if early:
        scratch += [pltpu.VMEM((2 * WIN, HD), jnp.bfloat16)] * 2
        scratch += [pltpu.VMEM((2 * WIN, HD), jnp.float32)] * 2
    grid_spec = pltpu.PrefetchScalarGridSpec(
        num_scalar_prefetch=1,
        grid=(block_count,),
        in_specs=in_specs,
        out_specs=[pl.BlockSpec((rows, 2 * HD), lambda b, f: (b + block_offset, 0))] * heads
        + [whole, whole]
        + ([pl.BlockSpec((WIN, 2 * HD), lambda b, f: (0, 0))] if early else []),
        scratch_shapes=scratch,
    )
    kernel = functools.partial(
        attend_kernel,
        heads=heads,
        block_offset=block_offset,
        early=early,
        carry_od=carry_od,
        acc_base=acc_base,
    )
    return pl.pallas_call(
        kernel,
        grid_spec=grid_spec,
        out_shape=[jax.ShapeDtypeStruct((query_count, 2 * HD), jnp.bfloat16)] * heads
        + [
            jax.ShapeDtypeStruct((acc_rows, HD), jnp.float32),
            jax.ShapeDtypeStruct((acc_rows, HD), jnp.float32),
        ]
        + ([jax.ShapeDtypeStruct((WIN, 2 * HD), jnp.bfloat16)] if early else []),
        input_output_aliases=aliases,
        compiler_params=pltpu.CompilerParams(
            dimension_semantics=("arbitrary",), vmem_limit_bytes=56 * 1024 * 1024
        ),
    )(*operands)


def exchange_in(pieces):
    stacked = jnp.transpose(jnp.concatenate(pieces, axis=-1), (1, 0, 2))
    moved = lax.all_to_all(stacked, "head", split_axis=0, concat_axis=0, tiled=True)
    return moved.reshape(moved.shape[0] * moved.shape[1], moved.shape[2])


def exchange_out(group_block):
    shared = lax.axis_size("head")
    split = group_block.reshape(shared, group_block.shape[0] // shared, group_block.shape[1])
    moved = lax.all_to_all(split, "head", split_axis=0, concat_axis=0, tiled=True)
    return jnp.transpose(moved, (1, 0, 2))


def body(queries, keys, values, grad_out):
    token_count = queries.shape[0]
    shared = KVH
    pair = (QH // KVH) * HD
    query_rows = queries.reshape(token_count, shared, pair)
    grad_rows = grad_out.reshape(token_count, shared, pair)
    key_rows = keys.reshape(token_count, shared, HD)
    value_rows = values.reshape(token_count, shared, HD)
    first_part = exchange_in(
        [key_rows, value_rows, query_rows[:, :, :HD], grad_rows[:, :, :HD]]
    )
    second_part = exchange_in([query_rows[:, :, HD:], grad_rows[:, :, HD:]])
    group_rows = first_part.shape[0]
    block_total = group_rows // BLK
    lead = WIN // BLK
    first_query = lax.axis_index("ctx") * group_rows
    tail = shifted(first_part[group_rows - WIN :, : 2 * HD], "ctx", 1)
    late = (lead, block_total - lead)
    early = (0, lead)
    head0 = (first_part, 2, 3)
    head1 = (second_part, 0, 1)
    first_out, key_late, value_late = attend([head0], first_part, None, first_query, late, (None,))
    first_out, second_out, key_early, value_early, halo_part = attend(
        [head0, head1], first_part, tail, first_query, early, (first_out, None)
    )
    back = shifted(halo_part, "ctx", -1).astype(jnp.float32)
    second_out, key_last, value_last = attend(
        [head1], first_part, None, first_query, late, (second_out,)
    )
    first_back = exchange_out(first_out)
    second_back = exchange_out(second_out)
    lead_pad = ((0, group_rows - WIN), (0, 0))
    tail_pad = ((group_rows - WIN, 0), (0, 0))
    key_grad = (
        key_late + key_last + jnp.pad(key_early, lead_pad) + jnp.pad(back[:, :HD], tail_pad)
    ).astype(jnp.bfloat16)
    value_grad = (
        value_late
        + value_last
        + jnp.pad(value_early, lead_pad)
        + jnp.pad(back[:, HD:], tail_pad)
    ).astype(jnp.bfloat16)
    grads_back = exchange_out(jnp.concatenate([key_grad, value_grad], axis=1))
    attended = jnp.concatenate([first_back[:, :, :HD], second_back[:, :, :HD]], axis=2)
    grad_queries = jnp.concatenate([first_back[:, :, HD:], second_back[:, :, HD:]], axis=2)
    return (
        attended.reshape(token_count, QH * HD),
        grad_queries.reshape(token_count, QH * HD),
        grads_back[:, :, :HD].reshape(token_count, KVH * HD),
        grads_back[:, :, HD:].reshape(token_count, KVH * HD),
    )


def solution(mesh):
    placed = (
        P(("ctx", "head"), None),
        P(("ctx", "head"), None),
        P(("ctx", "head"), None),
        P(("ctx", "head"), None),
    )
    return jax.shard_map(
        body,
        mesh=mesh,
        in_specs=placed,
        out_specs=(
            P(("ctx", "head"), None),
            P(("ctx", "head"), None),
            P(("ctx", "head"), None),
            P(("ctx", "head"), None),
        ),
        check_vma=False,
    )
```
